128 devices in a mesh: grp: 4 (over z_hi, core), dom: 32 (over x, z_lo, y).
Axes of the slice: x: 4, y: 4, z: 4 (z_hi: 2, z_lo: 2; z = z_hi * 2 + z_lo), core: 2. Of those that a mesh axis runs over, the one named last changes fastest.
Arguments:
- emb: bfloat16 [32, 4096, 256], P('dom', 'grp'), may hold values from -4.5 to 4.5
- rel: float32 [256], replicated, may hold values from 0.5 to 2
- round_key: int32 [1], replicated, may hold values from 1 to 31
- edge_src: int32 [4, 32, 16, 128], P('grp', 'dom'), may hold values from 0 to 4095
- edge_dst: int32 [4, 32, 16, 128], P('grp', 'dom'), may hold values from 0 to 4095
- neg_idx: int32 [4, 32, 16, 128], P('grp', 'dom'), may hold values from 0 to 4095
- block_count: int32 [4, 32, 2], P('grp', 'dom'), may hold values from 1 to 8
Outputs:
- emb_grad: float32 [32, 4096, 256], P('dom', 'grp')
The draws below stay inside these ranges and needn't reach their ends.
Inputs may be any that keep to these rules, and one draw needn't show every extreme that they name: Partition p is matched with partition p XOR round_key[0]; round_key is the same on every device. `edge_src`: row numbers within a partition. `edge_dst`: row numbers within a partition. `neg_idx`: row numbers within a partition.
All inputs are finite; a program needn't handle non-finite values.
Results may differ from the reference program's by a relative error of at most 0.009.
Values may be sent and summed in bfloat16 or wider, within the bound.
No kernel may reach another device: no remote copies, remote signals or barrier semaphores. Data moves between devices by JAX's collectives and lax.ppermute only.
A program may use at most 64 MiB of HBM per device.

```python
import math
import jax
import jax.numpy as jnp
from jax import lax

D = 256
NB = 8
EB = 128
PROWS = 4096
N_GRP = 4
N_DOM = 32


def draw_emb(key, part):
    first = jax.random.fold_in(key, 0)
    shape = (N_DOM, PROWS, D)
    values = jnp.clip(jax.random.normal(first, shape, jnp.float32), -4.0, 4.0)
    return jnp.clip(values, -4.5, 4.5).astype(jnp.bfloat16)


def place_ends(array, rng, low, largest):
    place = [jax.random.randint(jax.random.fold_in(rng, axis), (), 0, length) for axis, length in enumerate(array.shape)]
    longest = array.shape.index(max(array.shape))
    next_to = place[:longest] + [(place[longest] + 1) % array.shape[longest]] + place[longest + 1:]
    return array.at[tuple(place)].set(low).at[tuple(next_to)].set(largest)


def setup_inputs(seed: int = 0) -> dict:
    keys = jax.random.split(jax.random.key(seed), 8)
    return {
        "emb": draw_emb(jax.random.fold_in(keys[7], 71), 0),
        "rel": jnp.clip(jnp.exp(jax.random.uniform(keys[1], (D,), jnp.float32, math.log(0.5), math.log(2.0))), 0.5, 2.0),
        "round_key": jax.random.randint(keys[2], (1,), 1, N_DOM).astype(jnp.int32),
        "edge_src": place_ends(jax.random.randint(keys[3], (N_GRP, N_DOM, 2 * NB, EB), 0, PROWS), jax.random.fold_in(keys[3], 1), 0, PROWS - 1).astype(jnp.int32),
        "edge_dst": place_ends(jax.random.randint(keys[4], (N_GRP, N_DOM, 2 * NB, EB), 0, PROWS), jax.random.fold_in(keys[4], 1), 0, PROWS - 1).astype(jnp.int32),
        "neg_idx": place_ends(jax.random.randint(keys[5], (N_GRP, N_DOM, 2 * NB, EB), 0, PROWS), jax.random.fold_in(keys[5], 1), 0, PROWS - 1).astype(jnp.int32),
        "block_count": place_ends(jax.random.randint(keys[6], (N_GRP, N_DOM, 2), 1, NB + 1), jax.random.fold_in(keys[6], 1), 1, NB).astype(jnp.int32),
    }


def bucket_terms(src_table, dst_table, rel, src_idx, dst_idx, neg_idx, count):
    scale = D ** -0.5
    src_rows = src_table[src_idx]
    dst_rows = dst_table[dst_idx]
    neg_rows = dst_table[neg_idx]
    query = lax.optimization_barrier((src_rows * rel * scale).astype(jnp.bfloat16)).astype(jnp.float32)
    cand = jnp.concatenate([dst_rows, neg_rows], axis=1)
    logits = jnp.einsum('bed,bcd->bec', query, cand)
    probs = jax.nn.softmax(logits, axis=-1)
    live = (jnp.arange(NB, dtype=jnp.int32) < count).astype(jnp.float32)
    target = jnp.eye(EB, 2 * EB, dtype=jnp.float32)
    weights = ((probs - target) * live[:, None, None]).astype(jnp.bfloat16).astype(jnp.float32)
    grad_query = jnp.einsum('bec,bcd->bed', weights, cand)
    src_grad = (grad_query * rel * scale).astype(jnp.bfloat16).astype(jnp.float32)
    cand_grad = jnp.einsum('bec,bed->bcd', weights, query).astype(jnp.bfloat16).astype(jnp.float32)
    own = jnp.zeros((PROWS, D), jnp.float32).at[src_idx.reshape(-1)].add(src_grad.reshape(-1, D))
    far = jnp.zeros((PROWS, D), jnp.float32).at[dst_idx.reshape(-1)].add(cand_grad[:, :EB].reshape(-1, D))
    far = far.at[neg_idx.reshape(-1)].add(cand_grad[:, EB:].reshape(-1, D))
    return own, far


def reference(emb, rel, round_key, edge_src, edge_dst, neg_idx, block_count):
    table = emb.astype(jnp.float32)
    parts = jnp.arange(N_DOM, dtype=jnp.int32)
    partner = jnp.bitwise_xor(parts, round_key[0].astype(jnp.int32))

    def per_part(index):
        own_tab = table[index]
        mate_tab = table[partner[index]]

        def per_group(sources, targets, negatives, counts):
            own_a, far_a = bucket_terms(own_tab, own_tab, rel, sources[:NB], targets[:NB], negatives[:NB], counts[0])
            own_b, far_b = bucket_terms(own_tab, mate_tab, rel, sources[NB:], targets[NB:], negatives[NB:], counts[1])
            return own_a + own_b + far_a, far_b

        own_g, mate_g = jax.vmap(per_group)(edge_src[:, index], edge_dst[:, index], neg_idx[:, index], block_count[:, index])
        return jnp.sum(own_g, axis=0), jnp.sum(mate_g, axis=0)

    own_all, mate_all = lax.map(per_part, parts)
    return own_all + mate_all[partner]
```

```python
import jax
import jax.numpy as jnp
from jax import lax
from jax.sharding import PartitionSpec as P


def swap_with_partner(payload, round_key, axis):
    count = lax.axis_size(axis)

    def branch(key):
        route = [(i, i ^ key) for i in range(count)]
        return lambda x: jax.tree.map(lambda a: lax.ppermute(a, axis, route), x)

    branches = [branch(key) for key in range(1, count)]
    return lax.switch(round_key - 1, branches, payload)


def pick_rows(table, index):
    return jnp.take(table, index.reshape(-1), axis=0, mode="clip")


def add_rows(total, index, rows):
    return total.at[index.reshape(-1)].add(rows.astype(jnp.float32), mode="drop")


def block_grads(query, table, rel, dst_idx, neg_idx, count):
    blocks, width, depth = query.shape
    scale = depth ** (-0.5)
    dst_rows = pick_rows(table, dst_idx).reshape(blocks, width, depth)
    neg_rows = pick_rows(table, neg_idx).reshape(blocks, width, depth)
    cand = jnp.concatenate([dst_rows, neg_rows], axis=1)
    logits = jnp.einsum("bed,bcd->bec", query, cand, preferred_element_type=jnp.float32)
    probs = jax.nn.softmax(logits, axis=-1)
    live = (jnp.arange(blocks, dtype=jnp.int32) < count).astype(jnp.float32)
    target = jnp.eye(width, 2 * width, dtype=jnp.float32)
    weights = ((probs - target) * live[:, None, None]).astype(jnp.bfloat16)
    grad_query = jnp.einsum("bec,bcd->bed", weights, cand, preferred_element_type=jnp.float32)
    src_grad = (grad_query * rel * scale).astype(jnp.bfloat16)
    cand_grad = jnp.einsum(
        "bec,bed->bcd", weights, query, preferred_element_type=jnp.float32
    ).astype(jnp.bfloat16)
    return src_grad, cand_grad[:, :width], cand_grad[:, width:]


def on_device(emb, rel, round_key, edge_src, edge_dst, neg_idx, block_count):
    table = lax.all_gather(emb, "grp", axis=1, tiled=True)[0]
    rows, depth = table.shape
    scale = depth ** (-0.5)
    sources = edge_src[0, 0]
    targets = edge_dst[0, 0]
    negatives = neg_idx[0, 0]
    counts = block_count[0, 0]
    blocks = sources.shape[0] // 2
    width = sources.shape[1]

    src_rows = pick_rows(table, sources)
    query = (
        (src_rows.astype(jnp.float32) * rel * scale)
        .astype(jnp.bfloat16)
        .reshape(2 * blocks, width, depth)
    )
    sent = (query[blocks:], targets[blocks:], negatives[blocks:], counts[1:2])
    got_query, got_dst, got_neg, got_count = swap_with_partner(sent, round_key[0], "dom")

    sg_a, dg_a, ng_a = block_grads(
        query[:blocks], table, rel, targets[:blocks], negatives[:blocks], counts[0]
    )
    sg_m, dg_m, ng_m = block_grads(got_query, table, rel, got_dst, got_neg, got_count[0])
    sg_b = swap_with_partner(sg_m, round_key[0], "dom")

    total = jnp.zeros((rows, depth), jnp.float32)
    total = add_rows(total, sources[:blocks], sg_a.reshape(-1, depth))
    total = add_rows(total, sources[blocks:], sg_b.reshape(-1, depth))
    total = add_rows(total, targets[:blocks], dg_a.reshape(-1, depth))
    total = add_rows(total, negatives[:blocks], ng_a.reshape(-1, depth))
    total = add_rows(total, got_dst, dg_m.reshape(-1, depth))
    total = add_rows(total, got_neg, ng_m.reshape(-1, depth))
    return lax.psum_scatter(total[None], "grp", scatter_dimension=1, tiled=True)


def solution(mesh):
    return jax.shard_map(
        on_device,
        mesh=mesh,
        in_specs=(
            P("dom", "grp", None),
            P(),
            P(),
            P("grp", "dom", None, None),
            P("grp", "dom", None, None),
            P("grp", "dom", None, None),
            P("grp", "dom", None),
        ),
        out_specs=P("dom", "grp", None),
        check_vma=False,
    )
```

```python
import jax
import jax.numpy as jnp
from jax import lax
from jax.sharding import PartitionSpec as P


def swap_with_partner(payload, round_key, axis):
    count = lax.axis_size(axis)

    def branch(key):
        route = [(i, i ^ key) for i in range(count)]
        return lambda x: jax.tree.map(lambda a: lax.ppermute(a, axis, route), x)

    branches = [branch(key) for key in range(1, count)]
    return lax.switch(round_key - 1, branches, payload)


def one_hot(index, rows):
    flat = index.reshape(-1)
    return (flat[:, None] == jnp.arange(rows, dtype=jnp.int32)[None, :]).astype(jnp.bfloat16)


def pick_rows(table, index):
    hot = one_hot(index, table.shape[0])
    return jnp.dot(hot, table, preferred_element_type=jnp.float32).astype(jnp.bfloat16)


def pack_indices(parts, width):
    flat = jnp.concatenate([p.reshape(-1) for p in parts])
    halves = jnp.stack([jnp.right_shift(flat, 6), jnp.bitwise_and(flat, 63)])
    return halves.astype(jnp.bfloat16).reshape(-1, width)


def unpack_indices(packed, count, shape):
    halves = packed.reshape(2, -1).astype(jnp.int32)
    flat = halves[0] * 64 + halves[1]
    return [flat[i * flat.shape[0] // count:(i + 1) * flat.shape[0] // count].reshape(shape)
            for i in range(count)]


def block_grads(query, table, rel, dst_idx, neg_idx, count):
    blocks, width, depth = query.shape
    scale = depth ** (-0.5)
    dst_rows = pick_rows(table, dst_idx).reshape(blocks, width, depth)
    neg_rows = pick_rows(table, neg_idx).reshape(blocks, width, depth)
    cand = jnp.concatenate([dst_rows, neg_rows], axis=1)
    logits = jnp.einsum("bed,bcd->bec", query, cand, preferred_element_type=jnp.float32)
    probs = jax.nn.softmax(logits, axis=-1)
    live = (jnp.arange(blocks, dtype=jnp.int32) < count).astype(jnp.float32)
    target = jnp.eye(width, 2 * width, dtype=jnp.float32)
    weights = ((probs - target) * live[:, None, None]).astype(jnp.bfloat16)
    grad_query = jnp.einsum("bec,bcd->bed", weights, cand, preferred_element_type=jnp.float32)
    src_grad = (grad_query * rel * scale).astype(jnp.bfloat16)
    cand_grad = jnp.einsum(
        "bec,bed->bcd", weights, query, preferred_element_type=jnp.float32
    ).astype(jnp.bfloat16)
    return src_grad, cand_grad[:, :width], cand_grad[:, width:]


def on_device(emb, rel, round_key, edge_src, edge_dst, neg_idx, block_count):
    table = lax.all_gather(emb, "grp", axis=1, tiled=True)[0]
    rows, depth = table.shape
    scale = depth ** (-0.5)
    sources = edge_src[0, 0]
    targets = edge_dst[0, 0]
    negatives = neg_idx[0, 0]
    counts = block_count[0, 0]
    blocks = sources.shape[0] // 2
    width = sources.shape[1]

    src_rows = pick_rows(table, sources)
    query = (
        (src_rows.astype(jnp.float32) * rel * scale)
        .astype(jnp.bfloat16)
        .reshape(2 * blocks, width, depth)
    )
    packed = pack_indices([targets[blocks:], negatives[blocks:]], depth)
    tail = jnp.zeros((32 - packed.shape[0], depth), jnp.bfloat16)
    tail = tail.at[0].set(counts[1].astype(jnp.bfloat16))
    sent = jnp.concatenate([query[blocks:].reshape(-1, depth), packed, tail])
    got = swap_with_partner(sent, round_key[0], "dom")
    got_query = got[: blocks * width].reshape(blocks, width, depth)
    got_pack = got[blocks * width : blocks * width + packed.shape[0]]
    got_dst, got_neg = unpack_indices(got_pack, 2, (blocks, width))
    got_count = got[blocks * width + packed.shape[0], 0:1].astype(jnp.int32)

    sg_a, dg_a, ng_a = block_grads(
        query[:blocks], table, rel, targets[:blocks], negatives[:blocks], counts[0]
    )
    sg_m, dg_m, ng_m = block_grads(got_query, table, rel, got_dst, got_neg, got_count[0])
    sg_b = swap_with_partner(sg_m, round_key[0], "dom")

    where = jnp.concatenate(
        [sources.reshape(-1), targets[:blocks].reshape(-1), negatives[:blocks].reshape(-1),
         got_dst.reshape(-1), got_neg.reshape(-1)]
    )
    grads = jnp.concatenate(
        [g.reshape(-1, depth) for g in (sg_a, sg_b, dg_a, ng_a, dg_m, ng_m)]
    )
    total = jnp.einsum(
        "rp,rd->pd", one_hot(where, rows), grads, preferred_element_type=jnp.float32
    )
    return lax.psum_scatter(total[None], "grp", scatter_dimension=1, tiled=True)


def solution(mesh):
    return jax.shard_map(
        on_device,
        mesh=mesh,
        in_specs=(
            P("dom", "grp", None),
            P(),
            P(),
            P("grp", "dom", None, None),
            P("grp", "dom", None, None),
            P("grp", "dom", None, None),
            P("grp", "dom", None),
        ),
        out_specs=P("dom", "grp", None),
        check_vma=False,
    )
```

```python
import jax
import jax.numpy as jnp
from jax import lax
from jax.sharding import PartitionSpec as P

CHUNKS = 4


def swap_with_partner(payload, round_key, axis):
    count = lax.axis_size(axis)

    def branch(key):
        route = [(i, i ^ key) for i in range(count)]
        return lambda x: jax.tree.map(lambda a: lax.ppermute(a, axis, route), x)

    branches = [branch(key) for key in range(1, count)]
    return lax.switch(round_key - 1, branches, payload)


def one_hot(index, rows):
    flat = index.reshape(-1)
    return (flat[:, None] == jnp.arange(rows, dtype=jnp.int32)[None, :]).astype(jnp.bfloat16)


def pick_rows(table, index):
    hot = one_hot(index, table.shape[0])
    return jnp.dot(hot, table, preferred_element_type=jnp.float32).astype(jnp.bfloat16)


def pack_indices(parts, width):
    flat = jnp.concatenate([p.reshape(-1) for p in parts])
    halves = jnp.stack([jnp.right_shift(flat, 6), jnp.bitwise_and(flat, 63)])
    return halves.astype(jnp.bfloat16).reshape(-1, width)


def unpack_indices(packed, count, shape):
    halves = packed.reshape(2, -1).astype(jnp.int32)
    flat = halves[0] * 64 + halves[1]
    return [flat[i * flat.shape[0] // count:(i + 1) * flat.shape[0] // count].reshape(shape)
            for i in range(count)]


def block_grads(query, table, rel, dst_idx, neg_idx, count):
    blocks, width, depth = query.shape
    scale = depth ** (-0.5)
    dst_rows = pick_rows(table, dst_idx).reshape(blocks, width, depth)
    neg_rows = pick_rows(table, neg_idx).reshape(blocks, width, depth)
    cand = jnp.concatenate([dst_rows, neg_rows], axis=1)
    logits = jnp.einsum("bed,bcd->bec", query, cand, preferred_element_type=jnp.float32)
    probs = jax.nn.softmax(logits, axis=-1)
    live = (jnp.arange(blocks, dtype=jnp.int32) < count).astype(jnp.float32)
    target = jnp.eye(width, 2 * width, dtype=jnp.float32)
    weights = ((probs - target) * live[:, None, None]).astype(jnp.bfloat16)
    grad_query = jnp.einsum("bec,bcd->bed", weights, cand, preferred_element_type=jnp.float32)
    src_grad = (grad_query * rel * scale).astype(jnp.bfloat16)
    cand_grad = jnp.einsum(
        "bec,bed->bcd", weights, query, preferred_element_type=jnp.float32
    ).astype(jnp.bfloat16)
    return src_grad, cand_grad[:, :width], cand_grad[:, width:]


def on_device(emb, rel, round_key, edge_src, edge_dst, neg_idx, block_count):
    table = lax.all_gather(emb, "grp", axis=1, tiled=True)[0]
    rows, depth = table.shape
    scale = depth ** (-0.5)
    sources = edge_src[0, 0]
    targets = edge_dst[0, 0]
    negatives = neg_idx[0, 0]
    counts = block_count[0, 0]
    blocks = sources.shape[0] // 2
    width = sources.shape[1]

    src_rows = pick_rows(table, sources)
    query = (
        (src_rows.astype(jnp.float32) * rel * scale)
        .astype(jnp.bfloat16)
        .reshape(2 * blocks, width, depth)
    )
    packed = pack_indices([targets[blocks:], negatives[blocks:]], depth)
    tail = jnp.zeros((32 - packed.shape[0], depth), jnp.bfloat16)
    tail = tail.at[0].set(counts[1].astype(jnp.bfloat16))
    sent = jnp.concatenate([query[blocks:].reshape(-1, depth), packed, tail])
    got = swap_with_partner(sent, round_key[0], "dom")
    got_query = got[: blocks * width].reshape(blocks, width, depth)
    got_pack = got[blocks * width : blocks * width + packed.shape[0]]
    got_dst, got_neg = unpack_indices(got_pack, 2, (blocks, width))
    got_count = got[blocks * width + packed.shape[0], 0:1].astype(jnp.int32)

    sg_a, dg_a, ng_a = block_grads(
        query[:blocks], table, rel, targets[:blocks], negatives[:blocks], counts[0]
    )
    sg_m, dg_m, ng_m = block_grads(got_query, table, rel, got_dst, got_neg, got_count[0])
    sg_b = swap_with_partner(sg_m, round_key[0], "dom")

    where = jnp.concatenate(
        [sources.reshape(-1), targets[:blocks].reshape(-1), negatives[:blocks].reshape(-1),
         got_dst.reshape(-1), got_neg.reshape(-1)]
    )
    grads = jnp.concatenate(
        [g.reshape(-1, depth) for g in (sg_a, sg_b, dg_a, ng_a, dg_m, ng_m)]
    )
    owners = lax.axis_size("grp")
    share = rows // owners
    step = share // CHUNKS
    pieces = []
    for chunk in range(CHUNKS):
        picked = (
            jnp.arange(owners, dtype=jnp.int32)[:, None] * share
            + chunk * step
            + jnp.arange(step, dtype=jnp.int32)[None, :]
        ).reshape(-1)
        hot = (where[:, None] == picked[None, :]).astype(jnp.bfloat16)
        part = jnp.einsum("rp,rd->pd", hot, grads, preferred_element_type=jnp.float32)
        pieces.append(
            lax.psum_scatter(
                part.reshape(owners, step, depth), "grp", scatter_dimension=0, tiled=True
            ).reshape(step, depth)
        )
    return jnp.concatenate(pieces, axis=0)[None]


def solution(mesh):
    return jax.shard_map(
        on_device,
        mesh=mesh,
        in_specs=(
            P("dom", "grp", None),
            P(),
            P(),
            P("grp", "dom", None, None),
            P("grp", "dom", None, None),
            P("grp", "dom", None, None),
            P("grp", "dom", None),
        ),
        out_specs=P("dom", "grp", None),
        check_vma=False,
    )
```

```python
import jax
import jax.numpy as jnp
from jax import lax
from jax.sharding import PartitionSpec as P


def swap_with_partner(payload, round_key, axis):
    count = lax.axis_size(axis)

    def branch(key):
        route = [(i, i ^ key) for i in range(count)]
        return lambda x: jax.tree.map(lambda a: lax.ppermute(a, axis, route), x)

    branches = [branch(key) for key in range(1, count)]
    return lax.switch(round_key - 1, branches, payload)


def one_hot(index, rows):
    flat = index.reshape(-1)
    return (flat[:, None] == jnp.arange(rows, dtype=jnp.int32)[None, :]).astype(jnp.bfloat16)


def pick_rows(table, index):
    hot = one_hot(index, table.shape[0])
    return jnp.dot(hot, table, preferred_element_type=jnp.float32).astype(jnp.bfloat16)


def pack_indices(parts, width):
    flat = jnp.concatenate([p.reshape(-1) for p in parts])
    halves = jnp.stack([jnp.right_shift(flat, 6), jnp.bitwise_and(flat, 63)])
    return halves.astype(jnp.bfloat16).reshape(-1, width)


def unpack_indices(packed, count, shape):
    halves = packed.reshape(2, -1).astype(jnp.int32)
    flat = halves[0] * 64 + halves[1]
    return [flat[i * flat.shape[0] // count:(i + 1) * flat.shape[0] // count].reshape(shape)
            for i in range(count)]


def block_grads(query, table, rel, dst_idx, neg_idx, count):
    blocks, width, depth = query.shape
    scale = depth ** (-0.5)
    dst_rows = pick_rows(table, dst_idx).reshape(blocks, width, depth)
    neg_rows = pick_rows(table, neg_idx).reshape(blocks, width, depth)
    cand = jnp.concatenate([dst_rows, neg_rows], axis=1)
    logits = jnp.einsum("bed,bcd->bec", query, cand, preferred_element_type=jnp.float32)
    probs = jax.nn.softmax(logits, axis=-1)
    live = (jnp.arange(blocks, dtype=jnp.int32) < count).astype(jnp.float32)
    target = jnp.eye(width, 2 * width, dtype=jnp.float32)
    weights = ((probs - target) * live[:, None, None]).astype(jnp.bfloat16)
    grad_query = jnp.einsum("bec,bcd->bed", weights, cand, preferred_element_type=jnp.float32)
    src_grad = (grad_query * rel * scale).astype(jnp.bfloat16)
    cand_grad = jnp.einsum(
        "bec,bed->bcd", weights, query, preferred_element_type=jnp.float32
    ).astype(jnp.bfloat16)
    return src_grad, cand_grad[:, :width], cand_grad[:, width:]


def on_device(emb, rel, round_key, edge_src, edge_dst, neg_idx, block_count):
    table = lax.all_gather(emb, "grp", axis=1, tiled=True)[0]
    rows, depth = table.shape
    scale = depth ** (-0.5)
    sources = edge_src[0, 0]
    targets = edge_dst[0, 0]
    negatives = neg_idx[0, 0]
    counts = block_count[0, 0]
    blocks = sources.shape[0] // 2
    width = sources.shape[1]

    src_rows = pick_rows(table, sources)
    query = (
        (src_rows.astype(jnp.float32) * rel * scale)
        .astype(jnp.bfloat16)
        .reshape(2 * blocks, width, depth)
    )
    packed = pack_indices([targets[blocks:], negatives[blocks:]], depth)
    tail = jnp.zeros((32 - packed.shape[0], depth), jnp.bfloat16)
    tail = tail.at[0].set(counts[1].astype(jnp.bfloat16))
    sent = jnp.concatenate([query[blocks:].reshape(-1, depth), packed, tail])
    got = swap_with_partner(sent, round_key[0], "dom")
    got_query = got[: blocks * width].reshape(blocks, width, depth)
    got_pack = got[blocks * width : blocks * width + packed.shape[0]]
    got_dst, got_neg = unpack_indices(got_pack, 2, (blocks, width))
    got_count = got[blocks * width + packed.shape[0], 0:1].astype(jnp.int32)

    sg_a, dg_a, ng_a = block_grads(
        query[:blocks], table, rel, targets[:blocks], negatives[:blocks], counts[0]
    )
    sg_m, dg_m, ng_m = block_grads(got_query, table, rel, got_dst, got_neg, got_count[0])
    sg_b = swap_with_partner(sg_m, round_key[0], "dom")

    where = jnp.concatenate(
        [sources.reshape(-1), targets[:blocks].reshape(-1), negatives[:blocks].reshape(-1),
         got_dst.reshape(-1), got_neg.reshape(-1)]
    )
    grads = jnp.concatenate(
        [g.reshape(-1, depth) for g in (sg_a, sg_b, dg_a, ng_a, dg_m, ng_m)]
    )
    hot_t = (jnp.arange(rows, dtype=jnp.int32)[:, None] == where[None, :]).astype(jnp.bfloat16)
    total = jnp.dot(hot_t, grads, preferred_element_type=jnp.float32)
    return lax.psum_scatter(total[None], "grp", scatter_dimension=1, tiled=True)


def solution(mesh):
    return jax.shard_map(
        on_device,
        mesh=mesh,
        in_specs=(
            P("dom", "grp", None),
            P(),
            P(),
            P("grp", "dom", None, None),
            P("grp", "dom", None, None),
            P("grp", "dom", None, None),
            P("grp", "dom", None),
        ),
        out_specs=P("dom", "grp", None),
        check_vma=False,
    )
```

```python
import jax
import jax.numpy as jnp
from jax import lax
from jax.sharding import PartitionSpec as P


def swap_with_partner(payload, round_key, axis):
    count = lax.axis_size(axis)

    def branch(key):
        route = [(i, i ^ key) for i in range(count)]
        return lambda x: jax.tree.map(lambda a: lax.ppermute(a, axis, route), x)

    branches = [branch(key) for key in range(1, count)]
    return lax.switch(round_key - 1, branches, payload)


def one_hot(index, rows):
    flat = index.reshape(-1)
    return (flat[:, None] == jnp.arange(rows, dtype=jnp.int32)[None, :]).astype(jnp.bfloat16)


def pick_rows(table, index):
    hot = one_hot(index, table.shape[0])
    return jnp.dot(hot, table, preferred_element_type=jnp.float32).astype(jnp.bfloat16)


def pack_indices(parts, width):
    flat = jnp.concatenate([p.reshape(-1) for p in parts])
    halves = jnp.stack([jnp.right_shift(flat, 6), jnp.bitwise_and(flat, 63)])
    return halves.astype(jnp.bfloat16).reshape(-1, width)


def unpack_indices(packed, count, shape):
    halves = packed.reshape(2, -1).astype(jnp.int32)
    flat = halves[0] * 64 + halves[1]
    return [flat[i * flat.shape[0] // count:(i + 1) * flat.shape[0] // count].reshape(shape)
            for i in range(count)]


def block_grads(query, table, rel, dst_idx, neg_idx, count):
    blocks, width, depth = query.shape
    scale = depth ** (-0.5)
    dst_rows = pick_rows(table, dst_idx).reshape(blocks, width, depth)
    neg_rows = pick_rows(table, neg_idx).reshape(blocks, width, depth)
    cand = jnp.concatenate([dst_rows, neg_rows], axis=1)
    logits = jnp.einsum("bed,bcd->bec", query, cand, preferred_element_type=jnp.float32)
    probs = jax.nn.softmax(logits, axis=-1)
    live = (jnp.arange(blocks, dtype=jnp.int32) < count).astype(jnp.float32)
    target = jnp.eye(width, 2 * width, dtype=jnp.float32)
    weights = ((probs - target) * live[:, None, None]).astype(jnp.bfloat16)
    grad_query = jnp.einsum("bec,bcd->bed", weights, cand, preferred_element_type=jnp.float32)
    src_grad = (grad_query * rel * scale).astype(jnp.bfloat16)
    cand_grad = jnp.einsum(
        "bec,bed->bcd", weights, query, preferred_element_type=jnp.float32
    ).astype(jnp.bfloat16)
    return src_grad, cand_grad[:, :width], cand_grad[:, width:]


def on_device(emb, rel, round_key, edge_src, edge_dst, neg_idx, block_count):
    owners = lax.axis_size("grp")
    shard = emb[0]
    copies = jnp.broadcast_to(shard[None], (owners,) + shard.shape)
    table = lax.all_to_all(copies, "grp", 0, 0, tiled=True).reshape(-1, shard.shape[-1])
    rows, depth = table.shape
    scale = depth ** (-0.5)
    sources = edge_src[0, 0]
    targets = edge_dst[0, 0]
    negatives = neg_idx[0, 0]
    counts = block_count[0, 0]
    blocks = sources.shape[0] // 2
    width = sources.shape[1]

    src_rows = pick_rows(table, sources)
    query = (
        (src_rows.astype(jnp.float32) * rel * scale)
        .astype(jnp.bfloat16)
        .reshape(2 * blocks, width, depth)
    )
    packed = pack_indices([targets[blocks:], negatives[blocks:]], depth)
    tail = jnp.zeros((32 - packed.shape[0], depth), jnp.bfloat16)
    tail = tail.at[0].set(counts[1].astype(jnp.bfloat16))
    sent = jnp.concatenate([query[blocks:].reshape(-1, depth), packed, tail])
    got = swap_with_partner(sent, round_key[0], "dom")
    got_query = got[: blocks * width].reshape(blocks, width, depth)
    got_pack = got[blocks * width : blocks * width + packed.shape[0]]
    got_dst, got_neg = unpack_indices(got_pack, 2, (blocks, width))
    got_count = got[blocks * width + packed.shape[0], 0:1].astype(jnp.int32)

    sg_a, dg_a, ng_a = block_grads(
        query[:blocks], table, rel, targets[:blocks], negatives[:blocks], counts[0]
    )
    sg_m, dg_m, ng_m = block_grads(got_query, table, rel, got_dst, got_neg, got_count[0])
    sg_b = swap_with_partner(sg_m, round_key[0], "dom")

    where = jnp.concatenate(
        [sources.reshape(-1), targets[:blocks].reshape(-1), negatives[:blocks].reshape(-1),
         got_dst.reshape(-1), got_neg.reshape(-1)]
    )
    grads = jnp.concatenate(
        [g.reshape(-1, depth) for g in (sg_a, sg_b, dg_a, ng_a, dg_m, ng_m)]
    )
    hot_t = (jnp.arange(rows, dtype=jnp.int32)[:, None] == where[None, :]).astype(jnp.bfloat16)
    total = jnp.dot(hot_t, grads, preferred_element_type=jnp.float32)
    share = rows // owners
    me = lax.axis_index("grp")
    parts = total.reshape(owners, share, depth)
    got_parts = lax.all_to_all(parts.astype(jnp.bfloat16), "grp", 0, 0, tiled=True)
    own = lax.dynamic_slice_in_dim(total, me * share, share, axis=0)
    keep = (jnp.arange(owners, dtype=jnp.int32) == me)[:, None, None]
    summed = jnp.sum(jnp.where(keep, own[None], got_parts.astype(jnp.float32)), axis=0)
    return summed[None]


def solution(mesh):
    return jax.shard_map(
        on_device,
        mesh=mesh,
        in_specs=(
            P("dom", "grp", None),
            P(),
            P(),
            P("grp", "dom", None, None),
            P("grp", "dom", None, None),
            P("grp", "dom", None, None),
            P("grp", "dom", None),
        ),
        out_specs=P("dom", "grp", None),
        check_vma=False,
    )
```

```python
import jax
import jax.numpy as jnp
from jax import lax
from jax.sharding import PartitionSpec as P


def swap_with_partner(payload, round_key, axis):
    count = lax.axis_size(axis)
    shape = payload.shape
    pieces = payload.reshape((count, shape[0] // count) + shape[1:])
    spread = lax.all_to_all(pieces, axis, 0, 0, tiled=True)
    order = jnp.bitwise_xor(jnp.arange(count, dtype=jnp.int32), round_key)
    routed = jnp.take(spread, order, axis=0, mode="clip")
    return lax.all_to_all(routed, axis, 0, 0, tiled=True).reshape(shape)


def one_hot(index, rows):
    flat = index.reshape(-1)
    return (flat[:, None] == jnp.arange(rows, dtype=jnp.int32)[None, :]).astype(jnp.bfloat16)


def hot_rows(index, rows):
    flat = index.reshape(-1)
    return (jnp.arange(rows, dtype=jnp.int32)[:, None] == flat[None, :]).astype(jnp.bfloat16)


def pick_rows(table, index):
    hot = one_hot(index, table.shape[0])
    return jnp.dot(hot, table, preferred_element_type=jnp.float32).astype(jnp.bfloat16)


def pack_indices(parts, width):
    flat = jnp.concatenate([p.reshape(-1) for p in parts])
    halves = jnp.stack([jnp.right_shift(flat, 6), jnp.bitwise_and(flat, 63)])
    return halves.astype(jnp.bfloat16).reshape(-1, width)


def unpack_indices(packed, count, shape):
    halves = packed.reshape(2, -1).astype(jnp.int32)
    flat = halves[0] * 64 + halves[1]
    return [flat[i * flat.shape[0] // count:(i + 1) * flat.shape[0] // count].reshape(shape)
            for i in range(count)]


def block_grads(query, table, rel, dst_idx, neg_idx, count):
    blocks, width, depth = query.shape
    scale = depth ** (-0.5)
    dst_rows = pick_rows(table, dst_idx).reshape(blocks, width, depth)
    neg_rows = pick_rows(table, neg_idx).reshape(blocks, width, depth)
    cand = jnp.concatenate([dst_rows, neg_rows], axis=1)
    logits = jnp.einsum("bed,bcd->bec", query, cand, preferred_element_type=jnp.float32)
    probs = jax.nn.softmax(logits, axis=-1)
    live = (jnp.arange(blocks, dtype=jnp.int32) < count).astype(jnp.float32)
    target = jnp.eye(width, 2 * width, dtype=jnp.float32)
    weights = ((probs - target) * live[:, None, None]).astype(jnp.bfloat16)
    grad_query = jnp.einsum("bec,bcd->bed", weights, cand, preferred_element_type=jnp.float32)
    src_grad = (grad_query * rel * scale).astype(jnp.bfloat16)
    cand_grad = jnp.einsum(
        "bec,bed->bcd", weights, query, preferred_element_type=jnp.float32
    ).astype(jnp.bfloat16)
    return src_grad, cand_grad[:, :width], cand_grad[:, width:]


def on_device(emb, rel, round_key, edge_src, edge_dst, neg_idx, block_count):
    owners = lax.axis_size("grp")
    shard = emb[0]
    copies = jnp.broadcast_to(shard[None], (owners,) + shard.shape)
    table = lax.all_to_all(copies, "grp", 0, 0, tiled=True).reshape(-1, shard.shape[-1])
    rows, depth = table.shape
    scale = depth ** (-0.5)
    sources = edge_src[0, 0]
    targets = edge_dst[0, 0]
    negatives = neg_idx[0, 0]
    counts = block_count[0, 0]
    blocks = sources.shape[0] // 2
    width = sources.shape[1]

    src_rows = pick_rows(table, sources)
    query = (
        (src_rows.astype(jnp.float32) * rel * scale)
        .astype(jnp.bfloat16)
        .reshape(2 * blocks, width, depth)
    )
    packed = pack_indices([targets[blocks:], negatives[blocks:]], depth)
    tail = jnp.zeros((32 - packed.shape[0], depth), jnp.bfloat16)
    tail = tail.at[0].set(counts[1].astype(jnp.bfloat16))
    sent = jnp.concatenate([query[blocks:].reshape(-1, depth), packed, tail])
    got = swap_with_partner(sent, round_key[0], "dom")
    got_query = got[: blocks * width].reshape(blocks, width, depth)
    got_pack = got[blocks * width : blocks * width + packed.shape[0]]
    got_dst, got_neg = unpack_indices(got_pack, 2, (blocks, width))
    got_count = got[blocks * width + packed.shape[0], 0:1].astype(jnp.int32)

    sg_a, dg_a, ng_a = block_grads(
        query[:blocks], table, rel, targets[:blocks], negatives[:blocks], counts[0]
    )
    sg_m, dg_m, ng_m = block_grads(got_query, table, rel, got_dst, got_neg, got_count[0])
    sg_b = swap_with_partner(sg_m.reshape(-1, depth), round_key[0], "dom")

    where = jnp.concatenate(
        [sources[:blocks].reshape(-1), targets[:blocks].reshape(-1),
         negatives[:blocks].reshape(-1), got_dst.reshape(-1), got_neg.reshape(-1)]
    )
    grads = jnp.concatenate([g.reshape(-1, depth) for g in (sg_a, dg_a, ng_a, dg_m, ng_m)])
    total = jnp.dot(hot_rows(where, rows), grads, preferred_element_type=jnp.float32)
    total = total + jnp.dot(
        hot_rows(sources[blocks:], rows), sg_b.reshape(-1, depth),
        preferred_element_type=jnp.float32,
    )
    share = rows // owners
    me = lax.axis_index("grp")
    parts = total.reshape(owners, share, depth)
    got_parts = lax.all_to_all(parts.astype(jnp.bfloat16), "grp", 0, 0, tiled=True)
    own = lax.dynamic_slice_in_dim(total, me * share, share, axis=0)
    keep = (jnp.arange(owners, dtype=jnp.int32) == me)[:, None, None]
    summed = jnp.sum(jnp.where(keep, own[None], got_parts.astype(jnp.float32)), axis=0)
    return summed[None]


def solution(mesh):
    return jax.shard_map(
        on_device,
        mesh=mesh,
        in_specs=(
            P("dom", "grp", None),
            P(),
            P(),
            P("grp", "dom", None, None),
            P("grp", "dom", None, None),
            P("grp", "dom", None, None),
            P("grp", "dom", None),
        ),
        out_specs=P("dom", "grp", None),
        check_vma=False,
    )
```

```python
import jax
import jax.numpy as jnp
from jax import lax
from jax.sharding import PartitionSpec as P

HALVES = 2


def swap_with_partner(payload, round_key, axis):
    count = lax.axis_size(axis)

    def branch(key):
        route = [(i, i ^ key) for i in range(count)]
        return lambda x: jax.tree.map(lambda a: lax.ppermute(a, axis, route), x)

    branches = [branch(key) for key in range(1, count)]
    return lax.switch(round_key - 1, branches, payload)


def one_hot(index, rows):
    flat = index.reshape(-1)
    return (flat[:, None] == jnp.arange(rows, dtype=jnp.int32)[None, :]).astype(jnp.bfloat16)


def pick_rows(table, index):
    hot = one_hot(index, table.shape[0])
    return jnp.dot(hot, table, preferred_element_type=jnp.float32).astype(jnp.bfloat16)


def pack_indices(parts, width):
    flat = jnp.concatenate([p.reshape(-1) for p in parts])
    halves = jnp.stack([jnp.right_shift(flat, 6), jnp.bitwise_and(flat, 63)])
    return halves.astype(jnp.bfloat16).reshape(-1, width)


def unpack_indices(packed, count, shape):
    halves = packed.reshape(2, -1).astype(jnp.int32)
    flat = halves[0] * 64 + halves[1]
    return [flat[i * flat.shape[0] // count:(i + 1) * flat.shape[0] // count].reshape(shape)
            for i in range(count)]


def block_grads(query, table, rel, dst_idx, neg_idx, count):
    blocks, width, depth = query.shape
    scale = depth ** (-0.5)
    dst_rows = pick_rows(table, dst_idx).reshape(blocks, width, depth)
    neg_rows = pick_rows(table, neg_idx).reshape(blocks, width, depth)
    cand = jnp.concatenate([dst_rows, neg_rows], axis=1)
    logits = jnp.einsum("bed,bcd->bec", query, cand, preferred_element_type=jnp.float32)
    probs = jax.nn.softmax(logits, axis=-1)
    live = (jnp.arange(blocks, dtype=jnp.int32) < count).astype(jnp.float32)
    target = jnp.eye(width, 2 * width, dtype=jnp.float32)
    weights = ((probs - target) * live[:, None, None]).astype(jnp.bfloat16)
    grad_query = jnp.einsum("bec,bcd->bed", weights, cand, preferred_element_type=jnp.float32)
    src_grad = (grad_query * rel * scale).astype(jnp.bfloat16)
    cand_grad = jnp.einsum(
        "bec,bed->bcd", weights, query, preferred_element_type=jnp.float32
    ).astype(jnp.bfloat16)
    return src_grad, cand_grad[:, :width], cand_grad[:, width:]


def on_device(emb, rel, round_key, edge_src, edge_dst, neg_idx, block_count):
    owners = lax.axis_size("grp")
    shard = emb[0]
    copies = jnp.broadcast_to(shard[None], (owners,) + shard.shape)
    table = lax.all_to_all(copies, "grp", 0, 0, tiled=True).reshape(-1, shard.shape[-1])
    rows, depth = table.shape
    scale = depth ** (-0.5)
    sources = edge_src[0, 0]
    targets = edge_dst[0, 0]
    negatives = neg_idx[0, 0]
    counts = block_count[0, 0]
    blocks = sources.shape[0] // 2
    width = sources.shape[1]

    src_rows = pick_rows(table, sources)
    query = (
        (src_rows.astype(jnp.float32) * rel * scale)
        .astype(jnp.bfloat16)
        .reshape(2 * blocks, width, depth)
    )
    packed = pack_indices([targets[blocks:], negatives[blocks:]], depth)
    tail = jnp.zeros((32 - packed.shape[0], depth), jnp.bfloat16)
    tail = tail.at[0].set(counts[1].astype(jnp.bfloat16))
    sent = jnp.concatenate([query[blocks:].reshape(-1, depth), packed, tail])
    got = swap_with_partner(sent, round_key[0], "dom")
    got_query = got[: blocks * width].reshape(blocks, width, depth)
    got_pack = got[blocks * width : blocks * width + packed.shape[0]]
    got_dst, got_neg = unpack_indices(got_pack, 2, (blocks, width))
    got_count = got[blocks * width + packed.shape[0], 0:1].astype(jnp.int32)

    sg_a, dg_a, ng_a = block_grads(
        query[:blocks], table, rel, targets[:blocks], negatives[:blocks], counts[0]
    )
    sg_m, dg_m, ng_m = block_grads(got_query, table, rel, got_dst, got_neg, got_count[0])
    sg_b = swap_with_partner(sg_m, round_key[0], "dom")

    where = jnp.concatenate(
        [sources.reshape(-1), targets[:blocks].reshape(-1), negatives[:blocks].reshape(-1),
         got_dst.reshape(-1), got_neg.reshape(-1)]
    )
    grads = jnp.concatenate(
        [g.reshape(-1, depth) for g in (sg_a, sg_b, dg_a, ng_a, dg_m, ng_m)]
    )
    owners = lax.axis_size("grp")
    share = rows // owners
    step = share // HALVES
    me = lax.axis_index("grp")
    keep = (jnp.arange(owners, dtype=jnp.int32) == me)[:, None, None]
    pieces = []
    for half in range(HALVES):
        picked = (
            jnp.arange(owners, dtype=jnp.int32)[:, None] * share
            + half * step
            + jnp.arange(step, dtype=jnp.int32)[None, :]
        ).reshape(-1)
        hot_t = (picked[:, None] == where[None, :]).astype(jnp.bfloat16)
        part = jnp.dot(hot_t, grads, preferred_element_type=jnp.float32)
        part = part.reshape(owners, step, depth)
        got_parts = lax.all_to_all(part.astype(jnp.bfloat16), "grp", 0, 0, tiled=True)
        own = lax.dynamic_index_in_dim(part, me, axis=0)
        pieces.append(jnp.sum(jnp.where(keep, own, got_parts.astype(jnp.float32)), axis=0))
    return jnp.concatenate(pieces, axis=0)[None]


def solution(mesh):
    return jax.shard_map(
        on_device,
        mesh=mesh,
        in_specs=(
            P("dom", "grp", None),
            P(),
            P(),
            P("grp", "dom", None, None),
            P("grp", "dom", None, None),
            P("grp", "dom", None, None),
            P("grp", "dom", None),
        ),
        out_specs=P("dom", "grp", None),
        check_vma=False,
    )
```

```python
import jax
import jax.numpy as jnp
from jax import lax
from jax.sharding import PartitionSpec as P

HALVES = 2


def swap_with_partner(payload, round_key, axis):
    count = lax.axis_size(axis)

    def branch(key):
        route = [(i, i ^ key) for i in range(count)]
        return lambda x: jax.tree.map(lambda a: lax.ppermute(a, axis, route), x)

    branches = [branch(key) for key in range(1, count)]
    return lax.switch(round_key - 1, branches, payload)


def one_hot(index, rows):
    flat = index.reshape(-1)
    return (flat[:, None] == jnp.arange(rows, dtype=jnp.int32)[None, :]).astype(jnp.bfloat16)


def pick_rows(table, index):
    hot = one_hot(index, table.shape[0])
    return jnp.dot(hot, table, preferred_element_type=jnp.float32).astype(jnp.bfloat16)


def pack_indices(parts, width):
    flat = jnp.concatenate([p.reshape(-1) for p in parts])
    halves = jnp.stack([jnp.right_shift(flat, 6), jnp.bitwise_and(flat, 63)])
    return halves.astype(jnp.bfloat16).reshape(-1, width)


def unpack_indices(packed, count, shape):
    halves = packed.reshape(2, -1).astype(jnp.int32)
    flat = halves[0] * 64 + halves[1]
    return [flat[i * flat.shape[0] // count:(i + 1) * flat.shape[0] // count].reshape(shape)
            for i in range(count)]


def block_grads(query, dst_rows, neg_rows, rel, count):
    blocks, width, depth = query.shape
    scale = depth ** (-0.5)
    dst_rows = dst_rows.reshape(blocks, width, depth)
    neg_rows = neg_rows.reshape(blocks, width, depth)
    cand = jnp.concatenate([dst_rows, neg_rows], axis=1)
    logits = jnp.einsum("bed,bcd->bec", query, cand, preferred_element_type=jnp.float32)
    probs = jax.nn.softmax(logits, axis=-1)
    live = (jnp.arange(blocks, dtype=jnp.int32) < count).astype(jnp.float32)
    target = jnp.eye(width, 2 * width, dtype=jnp.float32)
    weights = ((probs - target) * live[:, None, None]).astype(jnp.bfloat16)
    grad_query = jnp.einsum("bec,bcd->bed", weights, cand, preferred_element_type=jnp.float32)
    src_grad = (grad_query * rel * scale).astype(jnp.bfloat16)
    cand_grad = jnp.einsum(
        "bec,bed->bcd", weights, query, preferred_element_type=jnp.float32
    ).astype(jnp.bfloat16)
    return src_grad, cand_grad[:, :width], cand_grad[:, width:]


def on_device(emb, rel, round_key, edge_src, edge_dst, neg_idx, block_count):
    owners = lax.axis_size("grp")
    shard = emb[0]
    copies = jnp.broadcast_to(shard[None], (owners,) + shard.shape)
    table = lax.all_to_all(copies, "grp", 0, 0, tiled=True).reshape(-1, shard.shape[-1])
    rows, depth = table.shape
    scale = depth ** (-0.5)
    sources = edge_src[0, 0]
    targets = edge_dst[0, 0]
    negatives = neg_idx[0, 0]
    counts = block_count[0, 0]
    blocks = sources.shape[0] // 2
    width = sources.shape[1]

    edges = blocks * width
    own_rows = pick_rows(
        table,
        jnp.concatenate(
            [sources.reshape(-1), targets[:blocks].reshape(-1), negatives[:blocks].reshape(-1)]
        ),
    )
    src_rows = own_rows[: 2 * edges]
    query = (
        (src_rows.astype(jnp.float32) * rel * scale)
        .astype(jnp.bfloat16)
        .reshape(2 * blocks, width, depth)
    )
    packed = pack_indices([targets[blocks:], negatives[blocks:]], depth)
    tail = jnp.zeros((32 - packed.shape[0], depth), jnp.bfloat16)
    tail = tail.at[0].set(counts[1].astype(jnp.bfloat16))
    sent = jnp.concatenate([query[blocks:].reshape(-1, depth), packed, tail])
    got = swap_with_partner(sent, round_key[0], "dom")
    got_query = got[: blocks * width].reshape(blocks, width, depth)
    got_pack = got[blocks * width : blocks * width + packed.shape[0]]
    got_dst, got_neg = unpack_indices(got_pack, 2, (blocks, width))
    got_count = got[blocks * width + packed.shape[0], 0:1].astype(jnp.int32)

    sg_a, dg_a, ng_a = block_grads(
        query[:blocks], own_rows[2 * edges : 3 * edges], own_rows[3 * edges :], rel, counts[0]
    )
    got_rows = pick_rows(table, jnp.concatenate([got_dst.reshape(-1), got_neg.reshape(-1)]))
    sg_m, dg_m, ng_m = block_grads(
        got_query, got_rows[:edges], got_rows[edges:], rel, got_count[0]
    )
    sg_b = swap_with_partner(sg_m, round_key[0], "dom")

    where = jnp.concatenate(
        [sources.reshape(-1), targets[:blocks].reshape(-1), negatives[:blocks].reshape(-1),
         got_dst.reshape(-1), got_neg.reshape(-1)]
    )
    grads = jnp.concatenate(
        [g.reshape(-1, depth) for g in (sg_a, sg_b, dg_a, ng_a, dg_m, ng_m)]
    )
    owners = lax.axis_size("grp")
    share = rows // owners
    step = share // HALVES
    me = lax.axis_index("grp")
    keep = (jnp.arange(owners, dtype=jnp.int32) == me)[:, None, None]
    pieces = []
    for half in range(HALVES):
        picked = (
            jnp.arange(owners, dtype=jnp.int32)[:, None] * share
            + half * step
            + jnp.arange(step, dtype=jnp.int32)[None, :]
        ).reshape(-1)
        hot_t = (picked[:, None] == where[None, :]).astype(jnp.bfloat16)
        part = jnp.dot(hot_t, grads, preferred_element_type=jnp.float32)
        part = part.reshape(owners, step, depth)
        got_parts = lax.all_to_all(part.astype(jnp.bfloat16), "grp", 0, 0, tiled=True)
        own = lax.dynamic_index_in_dim(part, me, axis=0)
        pieces.append(jnp.sum(jnp.where(keep, own, got_parts.astype(jnp.float32)), axis=0))
    return jnp.concatenate(pieces, axis=0)[None]


def solution(mesh):
    return jax.shard_map(
        on_device,
        mesh=mesh,
        in_specs=(
            P("dom", "grp", None),
            P(),
            P(),
            P("grp", "dom", None, None),
            P("grp", "dom", None, None),
            P("grp", "dom", None, None),
            P("grp", "dom", None),
        ),
        out_specs=P("dom", "grp", None),
        check_vma=False,
    )
```

```python
import jax
import jax.numpy as jnp
from jax import lax
from jax.sharding import PartitionSpec as P

HALVES = 2


def swap_with_partner(payload, round_key, axis):
    count = lax.axis_size(axis)

    def branch(key):
        route = [(i, i ^ key) for i in range(count)]
        return lambda x: jax.tree.map(lambda a: lax.ppermute(a, axis, route), x)

    branches = [branch(key) for key in range(1, count)]
    return lax.switch(round_key - 1, branches, payload)


def one_hot(index, rows):
    flat = index.reshape(-1)
    return (flat[:, None] == jnp.arange(rows, dtype=jnp.int32)[None, :]).astype(jnp.bfloat16)


def pick_rows(table, index):
    hot = one_hot(index, table.shape[0])
    return jnp.dot(hot, table, preferred_element_type=jnp.float32).astype(jnp.bfloat16)


def pack_indices(parts, width):
    flat = jnp.concatenate([p.reshape(-1) for p in parts])
    halves = jnp.stack([jnp.right_shift(flat, 6), jnp.bitwise_and(flat, 63)])
    return halves.astype(jnp.bfloat16).reshape(-1, width)


def unpack_indices(packed, count, shape):
    halves = packed.reshape(2, -1).astype(jnp.int32)
    flat = halves[0] * 64 + halves[1]
    return [flat[i * flat.shape[0] // count:(i + 1) * flat.shape[0] // count].reshape(shape)
            for i in range(count)]


def block_grads(query, dst_rows, neg_rows, rel, count):
    blocks, width, depth = query.shape
    scale = depth ** (-0.5)
    dst_rows = dst_rows.reshape(blocks, width, depth)
    neg_rows = neg_rows.reshape(blocks, width, depth)
    cand = jnp.concatenate([dst_rows, neg_rows], axis=1)
    logits = jnp.einsum("bed,bcd->bec", query, cand, preferred_element_type=jnp.float32)
    probs = jax.nn.softmax(logits, axis=-1)
    live = (jnp.arange(blocks, dtype=jnp.int32) < count).astype(jnp.float32)
    target = jnp.eye(width, 2 * width, dtype=jnp.float32)
    weights = ((probs - target) * live[:, None, None]).astype(jnp.bfloat16)
    grad_query = jnp.einsum("bec,bcd->bed", weights, cand, preferred_element_type=jnp.float32)
    src_grad = (grad_query * rel * scale).astype(jnp.bfloat16)
    cand_grad = jnp.einsum(
        "bec,bed->bcd", weights, query, preferred_element_type=jnp.float32
    ).astype(jnp.bfloat16)
    return src_grad, cand_grad[:, :width], cand_grad[:, width:]


def on_device(emb, rel, round_key, edge_src, edge_dst, neg_idx, block_count):
    owners = lax.axis_size("grp")
    shard = emb[0]
    ring = [shard] + [
        lax.ppermute(shard, "grp", [(i, (i + hop) % owners) for i in range(owners)])
        for hop in range(1, owners)
    ]
    table = jnp.concatenate(ring, axis=0)
    share = shard.shape[0]
    me = lax.axis_index("grp")

    def local(index):
        return (me - index // share) % owners * share + index % share

    rows, depth = table.shape
    scale = depth ** (-0.5)
    sources = edge_src[0, 0]
    targets = edge_dst[0, 0]
    negatives = neg_idx[0, 0]
    counts = block_count[0, 0]
    blocks = sources.shape[0] // 2
    width = sources.shape[1]

    edges = blocks * width
    own_idx = jnp.concatenate(
        [sources.reshape(-1), targets[:blocks].reshape(-1), negatives[:blocks].reshape(-1)]
    )
    own_rows = pick_rows(table, local(own_idx))
    src_rows = own_rows[: 2 * edges]
    query = (
        (src_rows.astype(jnp.float32) * rel * scale)
        .astype(jnp.bfloat16)
        .reshape(2 * blocks, width, depth)
    )
    packed = pack_indices([targets[blocks:], negatives[blocks:]], depth)
    tail = jnp.zeros((32 - packed.shape[0], depth), jnp.bfloat16)
    tail = tail.at[0].set(counts[1].astype(jnp.bfloat16))
    sent = jnp.concatenate([query[blocks:].reshape(-1, depth), packed, tail])
    got = swap_with_partner(sent, round_key[0], "dom")
    got_query = got[: blocks * width].reshape(blocks, width, depth)
    got_pack = got[blocks * width : blocks * width + packed.shape[0]]
    got_dst, got_neg = unpack_indices(got_pack, 2, (blocks, width))
    got_count = got[blocks * width + packed.shape[0], 0:1].astype(jnp.int32)

    sg_a, dg_a, ng_a = block_grads(
        query[:blocks], own_rows[2 * edges : 3 * edges], own_rows[3 * edges :], rel, counts[0]
    )
    got_rows = pick_rows(
        table, local(jnp.concatenate([got_dst.reshape(-1), got_neg.reshape(-1)]))
    )
    sg_m, dg_m, ng_m = block_grads(
        got_query, got_rows[:edges], got_rows[edges:], rel, got_count[0]
    )
    sg_b = swap_with_partner(sg_m, round_key[0], "dom")

    where = jnp.concatenate(
        [sources.reshape(-1), targets[:blocks].reshape(-1), negatives[:blocks].reshape(-1),
         got_dst.reshape(-1), got_neg.reshape(-1)]
    )
    grads = jnp.concatenate(
        [g.reshape(-1, depth) for g in (sg_a, sg_b, dg_a, ng_a, dg_m, ng_m)]
    )
    owners = lax.axis_size("grp")
    share = rows // owners
    step = share // HALVES
    me = lax.axis_index("grp")
    keep = (jnp.arange(owners, dtype=jnp.int32) == me)[:, None, None]
    pieces = []
    for half in range(HALVES):
        picked = (
            jnp.arange(owners, dtype=jnp.int32)[:, None] * share
            + half * step
            + jnp.arange(step, dtype=jnp.int32)[None, :]
        ).reshape(-1)
        hot_t = (picked[:, None] == where[None, :]).astype(jnp.bfloat16)
        part = jnp.dot(hot_t, grads, preferred_element_type=jnp.float32)
        part = part.reshape(owners, step, depth)
        got_parts = lax.all_to_all(part.astype(jnp.bfloat16), "grp", 0, 0, tiled=True)
        own = lax.dynamic_index_in_dim(part, me, axis=0)
        pieces.append(jnp.sum(jnp.where(keep, own, got_parts.astype(jnp.float32)), axis=0))
    return jnp.concatenate(pieces, axis=0)[None]


def solution(mesh):
    return jax.shard_map(
        on_device,
        mesh=mesh,
        in_specs=(
            P("dom", "grp", None),
            P(),
            P(),
            P("grp", "dom", None, None),
            P("grp", "dom", None, None),
            P("grp", "dom", None, None),
            P("grp", "dom", None),
        ),
        out_specs=P("dom", "grp", None),
        check_vma=False,
    )
```

```python
import jax
import jax.numpy as jnp
from jax import lax
from jax.sharding import PartitionSpec as P

HALVES = 1


def swap_with_partner(payload, round_key, axis):
    count = lax.axis_size(axis)

    def branch(key):
        route = [(i, i ^ key) for i in range(count)]
        return lambda x: jax.tree.map(lambda a: lax.ppermute(a, axis, route), x)

    branches = [branch(key) for key in range(1, count)]
    return lax.switch(round_key - 1, branches, payload)


def one_hot(index, rows):
    flat = index.reshape(-1)
    return (flat[:, None] == jnp.arange(rows, dtype=jnp.int32)[None, :]).astype(jnp.bfloat16)


def pick_rows(table, index):
    hot = one_hot(index, table.shape[0])
    return jnp.dot(hot, table, preferred_element_type=jnp.float32).astype(jnp.bfloat16)


def pack_indices(parts, width):
    flat = jnp.concatenate([p.reshape(-1) for p in parts])
    halves = jnp.stack([jnp.right_shift(flat, 6), jnp.bitwise_and(flat, 63)])
    return halves.astype(jnp.bfloat16).reshape(-1, width)


def unpack_indices(packed, count, shape):
    halves = packed.reshape(2, -1).astype(jnp.int32)
    flat = halves[0] * 64 + halves[1]
    return [flat[i * flat.shape[0] // count:(i + 1) * flat.shape[0] // count].reshape(shape)
            for i in range(count)]


def block_grads(query, dst_rows, neg_rows, rel, count):
    blocks, width, depth = query.shape
    scale = depth ** (-0.5)
    dst_rows = dst_rows.reshape(blocks, width, depth)
    neg_rows = neg_rows.reshape(blocks, width, depth)
    cand = jnp.concatenate([dst_rows, neg_rows], axis=1)
    logits = jnp.einsum("bed,bcd->bec", query, cand, preferred_element_type=jnp.float32)
    probs = jax.nn.softmax(logits, axis=-1)
    live = (jnp.arange(blocks, dtype=jnp.int32) < count).astype(jnp.float32)
    target = jnp.eye(width, 2 * width, dtype=jnp.float32)
    weights = ((probs - target) * live[:, None, None]).astype(jnp.bfloat16)
    grad_query = jnp.einsum("bec,bcd->bed", weights, cand, preferred_element_type=jnp.float32)
    src_grad = (grad_query * rel * scale).astype(jnp.bfloat16)
    cand_grad = jnp.einsum(
        "bec,bed->bcd", weights, query, preferred_element_type=jnp.float32
    ).astype(jnp.bfloat16)
    return src_grad, cand_grad[:, :width], cand_grad[:, width:]


def on_device(emb, rel, round_key, edge_src, edge_dst, neg_idx, block_count):
    owners = lax.axis_size("grp")
    shard = emb[0]
    copies = jnp.broadcast_to(shard[None], (owners,) + shard.shape)
    table = lax.all_to_all(copies, "grp", 0, 0, tiled=True).reshape(-1, shard.shape[-1])
    rows, depth = table.shape
    scale = depth ** (-0.5)
    sources = edge_src[0, 0]
    targets = edge_dst[0, 0]
    negatives = neg_idx[0, 0]
    counts = block_count[0, 0]
    blocks = sources.shape[0] // 2
    width = sources.shape[1]

    edges = blocks * width
    own_rows = pick_rows(
        table,
        jnp.concatenate(
            [sources.reshape(-1), targets[:blocks].reshape(-1), negatives[:blocks].reshape(-1)]
        ),
    )
    src_rows = own_rows[: 2 * edges]
    query = (
        (src_rows.astype(jnp.float32) * rel * scale)
        .astype(jnp.bfloat16)
        .reshape(2 * blocks, width, depth)
    )
    packed = pack_indices([targets[blocks:], negatives[blocks:]], depth)
    tail = jnp.zeros((32 - packed.shape[0], depth), jnp.bfloat16)
    tail = tail.at[0].set(counts[1].astype(jnp.bfloat16))
    sent = jnp.concatenate([query[blocks:].reshape(-1, depth), packed, tail])
    got = swap_with_partner(sent, round_key[0], "dom")
    got_query = got[: blocks * width].reshape(blocks, width, depth)
    got_pack = got[blocks * width : blocks * width + packed.shape[0]]
    got_dst, got_neg = unpack_indices(got_pack, 2, (blocks, width))
    got_count = got[blocks * width + packed.shape[0], 0:1].astype(jnp.int32)

    sg_a, dg_a, ng_a = block_grads(
        query[:blocks], own_rows[2 * edges : 3 * edges], own_rows[3 * edges :], rel, counts[0]
    )
    got_rows = pick_rows(table, jnp.concatenate([got_dst.reshape(-1), got_neg.reshape(-1)]))
    sg_m, dg_m, ng_m = block_grads(
        got_query, got_rows[:edges], got_rows[edges:], rel, got_count[0]
    )
    sg_b = swap_with_partner(sg_m, round_key[0], "dom")

    where = jnp.concatenate(
        [sources.reshape(-1), targets[:blocks].reshape(-1), negatives[:blocks].reshape(-1),
         got_dst.reshape(-1), got_neg.reshape(-1)]
    )
    grads = jnp.concatenate(
        [g.reshape(-1, depth) for g in (sg_a, sg_b, dg_a, ng_a, dg_m, ng_m)]
    )
    owners = lax.axis_size("grp")
    share = rows // owners
    step = share // HALVES
    me = lax.axis_index("grp")
    keep = (jnp.arange(owners, dtype=jnp.int32) == me)[:, None, None]
    pieces = []
    for half in range(HALVES):
        picked = (
            jnp.arange(owners, dtype=jnp.int32)[:, None] * share
            + half * step
            + jnp.arange(step, dtype=jnp.int32)[None, :]
        ).reshape(-1)
        hot_t = (picked[:, None] == where[None, :]).astype(jnp.bfloat16)
        part = jnp.dot(hot_t, grads, preferred_element_type=jnp.float32)
        part = part.reshape(owners, step, depth)
        got_parts = lax.all_to_all(part.astype(jnp.bfloat16), "grp", 0, 0, tiled=True)
        own = lax.dynamic_index_in_dim(part, me, axis=0)
        pieces.append(jnp.sum(jnp.where(keep, own, got_parts.astype(jnp.float32)), axis=0))
    return jnp.concatenate(pieces, axis=0)[None]


def solution(mesh):
    return jax.shard_map(
        on_device,
        mesh=mesh,
        in_specs=(
            P("dom", "grp", None),
            P(),
            P(),
            P("grp", "dom", None, None),
            P("grp", "dom", None, None),
            P("grp", "dom", None, None),
            P("grp", "dom", None),
        ),
        out_specs=P("dom", "grp", None),
        check_vma=False,
    )
```

```python
import jax
import jax.numpy as jnp
from jax import lax
from jax.sharding import PartitionSpec as P
from jax.experimental import pallas as pl


def swap_with_partner(payload, round_key, axis):
    count = lax.axis_size(axis)

    def branch(key):
        route = [(i, i ^ key) for i in range(count)]
        return lambda x: jax.tree.map(lambda a: lax.ppermute(a, axis, route), x)

    branches = [branch(key) for key in range(1, count)]
    return lax.switch(round_key - 1, branches, payload)


def one_hot(index, rows):
    flat = index.reshape(-1)
    return (flat[:, None] == jnp.arange(rows, dtype=jnp.int32)[None, :]).astype(jnp.bfloat16)


def pick_rows(table, index):
    hot = one_hot(index, table.shape[0])
    return jnp.dot(hot, table, preferred_element_type=jnp.float32).astype(jnp.bfloat16)


def scatter_rows(where, grads, rows, tile_rows=1024, tile_edges=2048):
    edges, depth = grads.shape

    def kernel(where_ref, grads_ref, out_ref):
        i = pl.program_id(0)

        @pl.when(pl.program_id(1) == 0)
        def _():
            out_ref[...] = jnp.zeros_like(out_ref)

        ids = i * tile_rows + lax.broadcasted_iota(jnp.int32, (tile_rows, tile_edges), 0)
        hot = (ids == where_ref[...]).astype(jnp.bfloat16)
        out_ref[...] += jnp.dot(hot, grads_ref[...], preferred_element_type=jnp.float32)

    return pl.pallas_call(
        kernel,
        grid=(rows // tile_rows, edges // tile_edges),
        in_specs=[
            pl.BlockSpec((1, tile_edges), lambda i, k: (0, k)),
            pl.BlockSpec((tile_edges, depth), lambda i, k: (k, 0)),
        ],
        out_specs=pl.BlockSpec((tile_rows, depth), lambda i, k: (i, 0)),
        out_shape=jax.ShapeDtypeStruct((rows, depth), jnp.float32),
        cost_estimate=pl.CostEstimate(
            flops=2 * rows * edges * depth,
            transcendentals=0,
            bytes_accessed=edges * depth * 2 + rows * depth * 4 + edges * 4,
        ),
    )(where.reshape(1, edges), grads)


def pack_indices(parts, width):
    flat = jnp.concatenate([p.reshape(-1) for p in parts])
    halves = jnp.stack([jnp.right_shift(flat, 6), jnp.bitwise_and(flat, 63)])
    return halves.astype(jnp.bfloat16).reshape(-1, width)


def unpack_indices(packed, count, shape):
    halves = packed.reshape(2, -1).astype(jnp.int32)
    flat = halves[0] * 64 + halves[1]
    return [flat[i * flat.shape[0] // count:(i + 1) * flat.shape[0] // count].reshape(shape)
            for i in range(count)]


def block_grads(query, dst_rows, neg_rows, rel, count):
    blocks, width, depth = query.shape
    scale = depth ** (-0.5)
    dst_rows = dst_rows.reshape(blocks, width, depth)
    neg_rows = neg_rows.reshape(blocks, width, depth)
    cand = jnp.concatenate([dst_rows, neg_rows], axis=1)
    logits = jnp.einsum("bed,bcd->bec", query, cand, preferred_element_type=jnp.float32)
    probs = jax.nn.softmax(logits, axis=-1)
    live = (jnp.arange(blocks, dtype=jnp.int32) < count).astype(jnp.float32)
    target = jnp.eye(width, 2 * width, dtype=jnp.float32)
    weights = ((probs - target) * live[:, None, None]).astype(jnp.bfloat16)
    grad_query = jnp.einsum("bec,bcd->bed", weights, cand, preferred_element_type=jnp.float32)
    src_grad = (grad_query * rel * scale).astype(jnp.bfloat16)
    cand_grad = jnp.einsum(
        "bec,bed->bcd", weights, query, preferred_element_type=jnp.float32
    ).astype(jnp.bfloat16)
    return src_grad, cand_grad[:, :width], cand_grad[:, width:]


def on_device(emb, rel, round_key, edge_src, edge_dst, neg_idx, block_count):
    owners = lax.axis_size("grp")
    shard = emb[0]
    copies = jnp.broadcast_to(shard[None], (owners,) + shard.shape)
    table = lax.all_to_all(copies, "grp", 0, 0, tiled=True).reshape(-1, shard.shape[-1])
    rows, depth = table.shape
    scale = depth ** (-0.5)
    sources = edge_src[0, 0]
    targets = edge_dst[0, 0]
    negatives = neg_idx[0, 0]
    counts = block_count[0, 0]
    blocks = sources.shape[0] // 2
    width = sources.shape[1]

    edges = blocks * width
    own_rows = pick_rows(
        table,
        jnp.concatenate(
            [sources.reshape(-1), targets[:blocks].reshape(-1), negatives[:blocks].reshape(-1)]
        ),
    )
    src_rows = own_rows[: 2 * edges]
    query = (
        (src_rows.astype(jnp.float32) * rel * scale)
        .astype(jnp.bfloat16)
        .reshape(2 * blocks, width, depth)
    )
    packed = pack_indices([targets[blocks:], negatives[blocks:]], depth)
    tail = jnp.zeros((32 - packed.shape[0], depth), jnp.bfloat16)
    tail = tail.at[0].set(counts[1].astype(jnp.bfloat16))
    sent = jnp.concatenate([query[blocks:].reshape(-1, depth), packed, tail])
    got = swap_with_partner(sent, round_key[0], "dom")
    got_query = got[: blocks * width].reshape(blocks, width, depth)
    got_pack = got[blocks * width : blocks * width + packed.shape[0]]
    got_dst, got_neg = unpack_indices(got_pack, 2, (blocks, width))
    got_count = got[blocks * width + packed.shape[0], 0:1].astype(jnp.int32)

    sg_a, dg_a, ng_a = block_grads(
        query[:blocks], own_rows[2 * edges : 3 * edges], own_rows[3 * edges :], rel, counts[0]
    )
    got_rows = pick_rows(table, jnp.concatenate([got_dst.reshape(-1), got_neg.reshape(-1)]))
    sg_m, dg_m, ng_m = block_grads(
        got_query, got_rows[:edges], got_rows[edges:], rel, got_count[0]
    )
    sg_b = swap_with_partner(sg_m, round_key[0], "dom")

    where = jnp.concatenate(
        [sources.reshape(-1), targets[:blocks].reshape(-1), negatives[:blocks].reshape(-1),
         got_dst.reshape(-1), got_neg.reshape(-1)]
    )
    grads = jnp.concatenate(
        [g.reshape(-1, depth) for g in (sg_a, sg_b, dg_a, ng_a, dg_m, ng_m)]
    )
    owners = lax.axis_size("grp")
    share = rows // owners
    me = lax.axis_index("grp")
    keep = (jnp.arange(owners, dtype=jnp.int32) == me)[:, None, None]
    part = scatter_rows(where, grads, rows).reshape(owners, share, depth)
    got_parts = lax.all_to_all(part.astype(jnp.bfloat16), "grp", 0, 0, tiled=True)
    own = lax.dynamic_index_in_dim(part, me, axis=0)
    return jnp.sum(jnp.where(keep, own, got_parts.astype(jnp.float32)), axis=0)[None]


def solution(mesh):
    return jax.shard_map(
        on_device,
        mesh=mesh,
        in_specs=(
            P("dom", "grp", None),
            P(),
            P(),
            P("grp", "dom", None, None),
            P("grp", "dom", None, None),
            P("grp", "dom", None, None),
            P("grp", "dom", None),
        ),
        out_specs=P("dom", "grp", None),
        check_vma=False,
    )
```

```python
import jax
import jax.numpy as jnp
from jax import lax
from jax.sharding import PartitionSpec as P
from jax.experimental import pallas as pl


def swap_with_partner(payload, round_key, axis):
    count = lax.axis_size(axis)

    def branch(key):
        route = [(i, i ^ key) for i in range(count)]
        return lambda x: jax.tree.map(lambda a: lax.ppermute(a, axis, route), x)

    branches = [branch(key) for key in range(1, count)]
    return lax.switch(round_key - 1, branches, payload)


def one_hot(index, rows):
    flat = index.reshape(-1)
    return (flat[:, None] == jnp.arange(rows, dtype=jnp.int32)[None, :]).astype(jnp.bfloat16)


def pick_rows(table, index):
    hot = one_hot(index, table.shape[0])
    return jnp.dot(hot, table, preferred_element_type=jnp.float32).astype(jnp.bfloat16)


def scatter_rows(where, grads, rows, tile_rows=1024, tile_edges=6144):
    edges, depth = grads.shape

    def kernel(where_ref, grads_ref, out_ref):
        i = pl.program_id(0)

        @pl.when(pl.program_id(1) == 0)
        def _():
            out_ref[...] = jnp.zeros_like(out_ref)

        ids = i * tile_rows + lax.broadcasted_iota(jnp.int32, (tile_rows, tile_edges), 0)
        hot = (ids == where_ref[...]).astype(jnp.bfloat16)
        out_ref[...] += jnp.dot(hot, grads_ref[...], preferred_element_type=jnp.float32)

    return pl.pallas_call(
        kernel,
        grid=(rows // tile_rows, edges // tile_edges),
        in_specs=[
            pl.BlockSpec((1, tile_edges), lambda i, k: (0, k)),
            pl.BlockSpec((tile_edges, depth), lambda i, k: (k, 0)),
        ],
        out_specs=pl.BlockSpec((tile_rows, depth), lambda i, k: (i, 0)),
        out_shape=jax.ShapeDtypeStruct((rows, depth), jnp.float32),
        cost_estimate=pl.CostEstimate(
            flops=2 * rows * edges * depth,
            transcendentals=0,
            bytes_accessed=edges * depth * 2 + rows * depth * 4 + edges * 4,
        ),
    )(where.reshape(1, edges), grads)


def pack_indices(parts, width):
    flat = jnp.concatenate([p.reshape(-1) for p in parts])
    halves = jnp.stack([jnp.right_shift(flat, 6), jnp.bitwise_and(flat, 63)])
    return halves.astype(jnp.bfloat16).reshape(-1, width)


def unpack_indices(packed, count, shape):
    halves = packed.reshape(2, -1).astype(jnp.int32)
    flat = halves[0] * 64 + halves[1]
    return [flat[i * flat.shape[0] // count:(i + 1) * flat.shape[0] // count].reshape(shape)
            for i in range(count)]


def block_grads(query, dst_rows, neg_rows, rel, count):
    blocks, width, depth = query.shape
    scale = depth ** (-0.5)
    dst_rows = dst_rows.reshape(blocks, width, depth)
    neg_rows = neg_rows.reshape(blocks, width, depth)
    cand = jnp.concatenate([dst_rows, neg_rows], axis=1)
    logits = jnp.einsum("bed,bcd->bec", query, cand, preferred_element_type=jnp.float32)
    probs = jax.nn.softmax(logits, axis=-1)
    live = (jnp.arange(blocks, dtype=jnp.int32) < count).astype(jnp.float32)
    target = jnp.eye(width, 2 * width, dtype=jnp.float32)
    weights = ((probs - target) * live[:, None, None]).astype(jnp.bfloat16)
    grad_query = jnp.einsum("bec,bcd->bed", weights, cand, preferred_element_type=jnp.float32)
    src_grad = (grad_query * rel * scale).astype(jnp.bfloat16)
    cand_grad = jnp.einsum(
        "bec,bed->bcd", weights, query, preferred_element_type=jnp.float32
    ).astype(jnp.bfloat16)
    return src_grad, cand_grad[:, :width], cand_grad[:, width:]


def on_device(emb, rel, round_key, edge_src, edge_dst, neg_idx, block_count):
    owners = lax.axis_size("grp")
    shard = emb[0]
    copies = jnp.broadcast_to(shard[None], (owners,) + shard.shape)
    table = lax.all_to_all(copies, "grp", 0, 0, tiled=True).reshape(-1, shard.shape[-1])
    rows, depth = table.shape
    scale = depth ** (-0.5)
    sources = edge_src[0, 0]
    targets = edge_dst[0, 0]
    negatives = neg_idx[0, 0]
    counts = block_count[0, 0]
    blocks = sources.shape[0] // 2
    width = sources.shape[1]

    edges = blocks * width
    own_rows = pick_rows(
        table,
        jnp.concatenate(
            [sources.reshape(-1), targets[:blocks].reshape(-1), negatives[:blocks].reshape(-1)]
        ),
    )
    src_rows = own_rows[: 2 * edges]
    query = (
        (src_rows.astype(jnp.float32) * rel * scale)
        .astype(jnp.bfloat16)
        .reshape(2 * blocks, width, depth)
    )
    packed = pack_indices([targets[blocks:], negatives[blocks:]], depth)
    tail = jnp.zeros((32 - packed.shape[0], depth), jnp.bfloat16)
    tail = tail.at[0].set(counts[1].astype(jnp.bfloat16))
    sent = jnp.concatenate([query[blocks:].reshape(-1, depth), packed, tail])
    got = swap_with_partner(sent, round_key[0], "dom")
    got_query = got[: blocks * width].reshape(blocks, width, depth)
    got_pack = got[blocks * width : blocks * width + packed.shape[0]]
    got_dst, got_neg = unpack_indices(got_pack, 2, (blocks, width))
    got_count = got[blocks * width + packed.shape[0], 0:1].astype(jnp.int32)

    sg_a, dg_a, ng_a = block_grads(
        query[:blocks], own_rows[2 * edges : 3 * edges], own_rows[3 * edges :], rel, counts[0]
    )
    got_rows = pick_rows(table, jnp.concatenate([got_dst.reshape(-1), got_neg.reshape(-1)]))
    sg_m, dg_m, ng_m = block_grads(
        got_query, got_rows[:edges], got_rows[edges:], rel, got_count[0]
    )
    sg_b = swap_with_partner(sg_m, round_key[0], "dom")

    where = jnp.concatenate(
        [sources.reshape(-1), targets[:blocks].reshape(-1), negatives[:blocks].reshape(-1),
         got_dst.reshape(-1), got_neg.reshape(-1)]
    )
    grads = jnp.concatenate(
        [g.reshape(-1, depth) for g in (sg_a, sg_b, dg_a, ng_a, dg_m, ng_m)]
    )
    owners = lax.axis_size("grp")
    share = rows // owners
    me = lax.axis_index("grp")
    keep = (jnp.arange(owners, dtype=jnp.int32) == me)[:, None, None]
    part = scatter_rows(where, grads, rows).reshape(owners, share, depth)
    got_parts = lax.all_to_all(part.astype(jnp.bfloat16), "grp", 0, 0, tiled=True)
    own = lax.dynamic_index_in_dim(part, me, axis=0)
    return jnp.sum(jnp.where(keep, own, got_parts.astype(jnp.float32)), axis=0)[None]


def solution(mesh):
    return jax.shard_map(
        on_device,
        mesh=mesh,
        in_specs=(
            P("dom", "grp", None),
            P(),
            P(),
            P("grp", "dom", None, None),
            P("grp", "dom", None, None),
            P("grp", "dom", None, None),
            P("grp", "dom", None),
        ),
        out_specs=P("dom", "grp", None),
        check_vma=False,
    )
```

```python
import jax
import jax.numpy as jnp
from jax import lax
from jax.sharding import PartitionSpec as P
from jax.experimental import pallas as pl


def swap_with_partner(payload, round_key, axis):
    count = lax.axis_size(axis)

    def branch(key):
        route = [(i, i ^ key) for i in range(count)]
        return lambda x: jax.tree.map(lambda a: lax.ppermute(a, axis, route), x)

    branches = [branch(key) for key in range(1, count)]
    return lax.switch(round_key - 1, branches, payload)


def one_hot(index, rows):
    flat = index.reshape(-1)
    return (flat[:, None] == jnp.arange(rows, dtype=jnp.int32)[None, :]).astype(jnp.bfloat16)


def pick_rows(table, index):
    hot = one_hot(index, table.shape[0])
    return jnp.dot(hot, table, preferred_element_type=jnp.float32).astype(jnp.bfloat16)


def scatter_rows(where, grads, rows, tile_rows=512, tile_edges=6144):
    edges, depth = grads.shape

    def kernel(where_ref, grads_ref, out_ref):
        i = pl.program_id(0)

        @pl.when(pl.program_id(1) == 0)
        def _():
            out_ref[...] = jnp.zeros_like(out_ref)

        ids = i * tile_rows + lax.broadcasted_iota(jnp.int32, (tile_rows, tile_edges), 0)
        hot = (ids == where_ref[...]).astype(jnp.bfloat16)
        out_ref[...] += jnp.dot(hot, grads_ref[...], preferred_element_type=jnp.float32)

    return pl.pallas_call(
        kernel,
        grid=(rows // tile_rows, edges // tile_edges),
        in_specs=[
            pl.BlockSpec((1, tile_edges), lambda i, k: (0, k)),
            pl.BlockSpec((tile_edges, depth), lambda i, k: (k, 0)),
        ],
        out_specs=pl.BlockSpec((tile_rows, depth), lambda i, k: (i, 0)),
        out_shape=jax.ShapeDtypeStruct((rows, depth), jnp.float32),
        cost_estimate=pl.CostEstimate(
            flops=2 * rows * edges * depth,
            transcendentals=0,
            bytes_accessed=edges * depth * 2 + rows * depth * 4 + edges * 4,
        ),
    )(where.reshape(1, edges), grads)


def pack_indices(parts, width):
    flat = jnp.concatenate([p.reshape(-1) for p in parts])
    halves = jnp.stack([jnp.right_shift(flat, 6), jnp.bitwise_and(flat, 63)])
    return halves.astype(jnp.bfloat16).reshape(-1, width)


def unpack_indices(packed, count, shape):
    halves = packed.reshape(2, -1).astype(jnp.int32)
    flat = halves[0] * 64 + halves[1]
    return [flat[i * flat.shape[0] // count:(i + 1) * flat.shape[0] // count].reshape(shape)
            for i in range(count)]


def block_grads(query, dst_rows, neg_rows, rel, count):
    blocks, width, depth = query.shape
    scale = depth ** (-0.5)
    dst_rows = dst_rows.reshape(blocks, width, depth)
    neg_rows = neg_rows.reshape(blocks, width, depth)
    cand = jnp.concatenate([dst_rows, neg_rows], axis=1)
    logits = jnp.einsum("bed,bcd->bec", query, cand, preferred_element_type=jnp.float32)
    probs = jax.nn.softmax(logits, axis=-1)
    live = (jnp.arange(blocks, dtype=jnp.int32) < count).astype(jnp.float32)
    target = jnp.eye(width, 2 * width, dtype=jnp.float32)
    weights = ((probs - target) * live[:, None, None]).astype(jnp.bfloat16)
    grad_query = jnp.einsum("bec,bcd->bed", weights, cand, preferred_element_type=jnp.float32)
    src_grad = (grad_query * rel * scale).astype(jnp.bfloat16)
    cand_grad = jnp.einsum(
        "bec,bed->bcd", weights, query, preferred_element_type=jnp.float32
    ).astype(jnp.bfloat16)
    return src_grad, cand_grad[:, :width], cand_grad[:, width:]


def on_device(emb, rel, round_key, edge_src, edge_dst, neg_idx, block_count):
    owners = lax.axis_size("grp")
    shard = emb[0]
    copies = jnp.broadcast_to(shard[None], (owners,) + shard.shape)
    table = lax.all_to_all(copies, "grp", 0, 0, tiled=True).reshape(-1, shard.shape[-1])
    rows, depth = table.shape
    scale = depth ** (-0.5)
    sources = edge_src[0, 0]
    targets = edge_dst[0, 0]
    negatives = neg_idx[0, 0]
    counts = block_count[0, 0]
    blocks = sources.shape[0] // 2
    width = sources.shape[1]

    edges = blocks * width
    own_rows = pick_rows(
        table,
        jnp.concatenate(
            [sources.reshape(-1), targets[:blocks].reshape(-1), negatives[:blocks].reshape(-1)]
        ),
    )
    src_rows = own_rows[: 2 * edges]
    query = (
        (src_rows.astype(jnp.float32) * rel * scale)
        .astype(jnp.bfloat16)
        .reshape(2 * blocks, width, depth)
    )
    packed = pack_indices([targets[blocks:], negatives[blocks:]], depth)
    tail = jnp.zeros((32 - packed.shape[0], depth), jnp.bfloat16)
    tail = tail.at[0].set(counts[1].astype(jnp.bfloat16))
    sent = jnp.concatenate([query[blocks:].reshape(-1, depth), packed, tail])
    got = swap_with_partner(sent, round_key[0], "dom")
    got_query = got[: blocks * width].reshape(blocks, width, depth)
    got_pack = got[blocks * width : blocks * width + packed.shape[0]]
    got_dst, got_neg = unpack_indices(got_pack, 2, (blocks, width))
    got_count = got[blocks * width + packed.shape[0], 0:1].astype(jnp.int32)

    sg_a, dg_a, ng_a = block_grads(
        query[:blocks], own_rows[2 * edges : 3 * edges], own_rows[3 * edges :], rel, counts[0]
    )
    got_rows = pick_rows(table, jnp.concatenate([got_dst.reshape(-1), got_neg.reshape(-1)]))
    sg_m, dg_m, ng_m = block_grads(
        got_query, got_rows[:edges], got_rows[edges:], rel, got_count[0]
    )
    sg_b = swap_with_partner(sg_m, round_key[0], "dom")

    where = jnp.concatenate(
        [sources.reshape(-1), targets[:blocks].reshape(-1), negatives[:blocks].reshape(-1),
         got_dst.reshape(-1), got_neg.reshape(-1)]
    )
    grads = jnp.concatenate(
        [g.reshape(-1, depth) for g in (sg_a, sg_b, dg_a, ng_a, dg_m, ng_m)]
    )
    owners = lax.axis_size("grp")
    share = rows // owners
    me = lax.axis_index("grp")
    keep = (jnp.arange(owners, dtype=jnp.int32) == me)[:, None, None]
    part = scatter_rows(where, grads, rows).reshape(owners, share, depth)
    got_parts = lax.all_to_all(part.astype(jnp.bfloat16), "grp", 0, 0, tiled=True)
    own = lax.dynamic_index_in_dim(part, me, axis=0)
    return jnp.sum(jnp.where(keep, own, got_parts.astype(jnp.float32)), axis=0)[None]


def solution(mesh):
    return jax.shard_map(
        on_device,
        mesh=mesh,
        in_specs=(
            P("dom", "grp", None),
            P(),
            P(),
            P("grp", "dom", None, None),
            P("grp", "dom", None, None),
            P("grp", "dom", None, None),
            P("grp", "dom", None),
        ),
        out_specs=P("dom", "grp", None),
        check_vma=False,
    )
```

```python
import jax
import jax.numpy as jnp
from jax import lax
from jax.sharding import PartitionSpec as P
from jax.experimental import pallas as pl


def swap_with_partner(payload, round_key, axis):
    count = lax.axis_size(axis)

    def branch(key):
        route = [(i, i ^ key) for i in range(count)]
        return lambda x: jax.tree.map(lambda a: lax.ppermute(a, axis, route), x)

    branches = [branch(key) for key in range(1, count)]
    return lax.switch(round_key - 1, branches, payload)


def one_hot(index, rows):
    flat = index.reshape(-1)
    return (flat[:, None] == jnp.arange(rows, dtype=jnp.int32)[None, :]).astype(jnp.bfloat16)


def pick_rows(table, index):
    hot = one_hot(index, table.shape[0])
    return jnp.dot(hot, table, preferred_element_type=jnp.float32).astype(jnp.bfloat16)


def scatter_rows(where, grads, rows, tile_rows=512):
    edges, depth = grads.shape

    def kernel(where_ref, grads_ref, out_ref, low_ref):
        ids = pl.program_id(0) * tile_rows + lax.broadcasted_iota(
            jnp.int32, (tile_rows, edges), 0
        )
        hot = (ids == where_ref[...]).astype(jnp.bfloat16)
        total = jnp.dot(hot, grads_ref[...], preferred_element_type=jnp.float32)
        out_ref[...] = total
        low_ref[...] = total.astype(jnp.bfloat16)

    return pl.pallas_call(
        kernel,
        grid=(rows // tile_rows,),
        in_specs=[
            pl.BlockSpec((1, edges), lambda i: (0, 0)),
            pl.BlockSpec((edges, depth), lambda i: (0, 0)),
        ],
        out_specs=[
            pl.BlockSpec((tile_rows, depth), lambda i: (i, 0)),
            pl.BlockSpec((tile_rows, depth), lambda i: (i, 0)),
        ],
        out_shape=[
            jax.ShapeDtypeStruct((rows, depth), jnp.float32),
            jax.ShapeDtypeStruct((rows, depth), jnp.bfloat16),
        ],
        cost_estimate=pl.CostEstimate(
            flops=2 * rows * edges * depth,
            transcendentals=0,
            bytes_accessed=edges * depth * 2 + rows * depth * 6 + edges * 4,
        ),
    )(where.reshape(1, edges), grads)


def pack_indices(parts, width):
    flat = jnp.concatenate([p.reshape(-1) for p in parts])
    halves = jnp.stack([jnp.right_shift(flat, 6), jnp.bitwise_and(flat, 63)])
    return halves.astype(jnp.bfloat16).reshape(-1, width)


def unpack_indices(packed, count, shape):
    halves = packed.reshape(2, -1).astype(jnp.int32)
    flat = halves[0] * 64 + halves[1]
    return [flat[i * flat.shape[0] // count:(i + 1) * flat.shape[0] // count].reshape(shape)
            for i in range(count)]


def block_grads(query, dst_rows, neg_rows, rel, count):
    blocks, width, depth = query.shape
    scale = depth ** (-0.5)
    dst_rows = dst_rows.reshape(blocks, width, depth)
    neg_rows = neg_rows.reshape(blocks, width, depth)
    cand = jnp.concatenate([dst_rows, neg_rows], axis=1)
    logits = jnp.einsum("bed,bcd->bec", query, cand, preferred_element_type=jnp.float32)
    probs = jax.nn.softmax(logits, axis=-1)
    live = (jnp.arange(blocks, dtype=jnp.int32) < count).astype(jnp.float32)
    target = jnp.eye(width, 2 * width, dtype=jnp.float32)
    weights = ((probs - target) * live[:, None, None]).astype(jnp.bfloat16)
    grad_query = jnp.einsum("bec,bcd->bed", weights, cand, preferred_element_type=jnp.float32)
    src_grad = (grad_query * rel * scale).astype(jnp.bfloat16)
    cand_grad = jnp.einsum(
        "bec,bed->bcd", weights, query, preferred_element_type=jnp.float32
    ).astype(jnp.bfloat16)
    return src_grad, cand_grad[:, :width], cand_grad[:, width:]


def on_device(emb, rel, round_key, edge_src, edge_dst, neg_idx, block_count):
    owners = lax.axis_size("grp")
    shard = emb[0]
    copies = jnp.broadcast_to(shard[None], (owners,) + shard.shape)
    table = lax.all_to_all(copies, "grp", 0, 0, tiled=True).reshape(-1, shard.shape[-1])
    rows, depth = table.shape
    scale = depth ** (-0.5)
    sources = edge_src[0, 0]
    targets = edge_dst[0, 0]
    negatives = neg_idx[0, 0]
    counts = block_count[0, 0]
    blocks = sources.shape[0] // 2
    width = sources.shape[1]

    edges = blocks * width
    own_rows = pick_rows(
        table,
        jnp.concatenate(
            [sources.reshape(-1), targets[:blocks].reshape(-1), negatives[:blocks].reshape(-1)]
        ),
    )
    src_rows = own_rows[: 2 * edges]
    query = (
        (src_rows.astype(jnp.float32) * rel * scale)
        .astype(jnp.bfloat16)
        .reshape(2 * blocks, width, depth)
    )
    packed = pack_indices([targets[blocks:], negatives[blocks:]], depth)
    tail = jnp.zeros((32 - packed.shape[0], depth), jnp.bfloat16)
    tail = tail.at[0].set(counts[1].astype(jnp.bfloat16))
    sent = jnp.concatenate([query[blocks:].reshape(-1, depth), packed, tail])
    got = swap_with_partner(sent, round_key[0], "dom")
    got_query = got[: blocks * width].reshape(blocks, width, depth)
    got_pack = got[blocks * width : blocks * width + packed.shape[0]]
    got_dst, got_neg = unpack_indices(got_pack, 2, (blocks, width))
    got_count = got[blocks * width + packed.shape[0], 0:1].astype(jnp.int32)

    sg_a, dg_a, ng_a = block_grads(
        query[:blocks], own_rows[2 * edges : 3 * edges], own_rows[3 * edges :], rel, counts[0]
    )
    got_rows = pick_rows(table, jnp.concatenate([got_dst.reshape(-1), got_neg.reshape(-1)]))
    sg_m, dg_m, ng_m = block_grads(
        got_query, got_rows[:edges], got_rows[edges:], rel, got_count[0]
    )
    sg_b = swap_with_partner(sg_m, round_key[0], "dom")

    where = jnp.concatenate(
        [sources.reshape(-1), targets[:blocks].reshape(-1), negatives[:blocks].reshape(-1),
         got_dst.reshape(-1), got_neg.reshape(-1)]
    )
    grads = jnp.concatenate(
        [g.reshape(-1, depth) for g in (sg_a, sg_b, dg_a, ng_a, dg_m, ng_m)]
    )
    owners = lax.axis_size("grp")
    share = rows // owners
    me = lax.axis_index("grp")
    keep = (jnp.arange(owners, dtype=jnp.int32) == me)[:, None, None]
    part, low = scatter_rows(where, grads, rows)
    part = part.reshape(owners, share, depth)
    got_parts = lax.all_to_all(low.reshape(owners, share, depth), "grp", 0, 0, tiled=True)
    own = lax.dynamic_index_in_dim(part, me, axis=0)
    return jnp.sum(jnp.where(keep, own, got_parts.astype(jnp.float32)), axis=0)[None]


def solution(mesh):
    return jax.shard_map(
        on_device,
        mesh=mesh,
        in_specs=(
            P("dom", "grp", None),
            P(),
            P(),
            P("grp", "dom", None, None),
            P("grp", "dom", None, None),
            P("grp", "dom", None, None),
            P("grp", "dom", None),
        ),
        out_specs=P("dom", "grp", None),
        check_vma=False,
    )
```

```python
import jax
import jax.numpy as jnp
from jax import lax
from jax.sharding import PartitionSpec as P
from jax.experimental import pallas as pl


def swap_with_partner(payload, round_key, axis):
    count = lax.axis_size(axis)

    def branch(key):
        route = [(i, i ^ key) for i in range(count)]
        return lambda x: jax.tree.map(lambda a: lax.ppermute(a, axis, route), x)

    branches = [branch(key) for key in range(1, count)]
    return lax.switch(round_key - 1, branches, payload)


def one_hot(index, rows):
    flat = index.reshape(-1)
    return (flat[:, None] == jnp.arange(rows, dtype=jnp.int32)[None, :]).astype(jnp.bfloat16)


def pick_rows(table, index):
    hot = one_hot(index, table.shape[0])
    return jnp.dot(hot, table, preferred_element_type=jnp.float32).astype(jnp.bfloat16)


def scatter_rows(where, grads, rows, tile_rows=256):
    edges, depth = grads.shape

    def kernel(where_ref, grads_ref, out_ref, low_ref):
        ids = pl.program_id(0) * tile_rows + lax.broadcasted_iota(
            jnp.int32, (tile_rows, edges), 0
        )
        hot = (ids == where_ref[...]).astype(jnp.bfloat16)
        total = jnp.dot(hot, grads_ref[...], preferred_element_type=jnp.float32)
        out_ref[...] = total
        low_ref[...] = total.astype(jnp.bfloat16)

    return pl.pallas_call(
        kernel,
        grid=(rows // tile_rows,),
        in_specs=[
            pl.BlockSpec((1, edges), lambda i: (0, 0)),
            pl.BlockSpec((edges, depth), lambda i: (0, 0)),
        ],
        out_specs=[
            pl.BlockSpec((tile_rows, depth), lambda i: (i, 0)),
            pl.BlockSpec((tile_rows, depth), lambda i: (i, 0)),
        ],
        out_shape=[
            jax.ShapeDtypeStruct((rows, depth), jnp.float32),
            jax.ShapeDtypeStruct((rows, depth), jnp.bfloat16),
        ],
        cost_estimate=pl.CostEstimate(
            flops=2 * rows * edges * depth,
            transcendentals=0,
            bytes_accessed=edges * depth * 2 + rows * depth * 6 + edges * 4,
        ),
    )(where.reshape(1, edges), grads)


def pack_indices(parts, width):
    flat = jnp.concatenate([p.reshape(-1) for p in parts])
    halves = jnp.stack([jnp.right_shift(flat, 6), jnp.bitwise_and(flat, 63)])
    return halves.astype(jnp.bfloat16).reshape(-1, width)


def unpack_indices(packed, count, shape):
    halves = packed.reshape(2, -1).astype(jnp.int32)
    flat = halves[0] * 64 + halves[1]
    return [flat[i * flat.shape[0] // count:(i + 1) * flat.shape[0] // count].reshape(shape)
            for i in range(count)]


def block_grads(query, dst_rows, neg_rows, rel, count):
    blocks, width, depth = query.shape
    scale = depth ** (-0.5)
    dst_rows = dst_rows.reshape(blocks, width, depth)
    neg_rows = neg_rows.reshape(blocks, width, depth)
    cand = jnp.concatenate([dst_rows, neg_rows], axis=1)
    logits = jnp.einsum("bed,bcd->bec", query, cand, preferred_element_type=jnp.float32)
    probs = jax.nn.softmax(logits, axis=-1)
    live = (jnp.arange(blocks, dtype=jnp.int32) < count).astype(jnp.float32)
    target = jnp.eye(width, 2 * width, dtype=jnp.float32)
    weights = ((probs - target) * live[:, None, None]).astype(jnp.bfloat16)
    grad_query = jnp.einsum("bec,bcd->bed", weights, cand, preferred_element_type=jnp.float32)
    src_grad = (grad_query * rel * scale).astype(jnp.bfloat16)
    cand_grad = jnp.einsum(
        "bec,bed->bcd", weights, query, preferred_element_type=jnp.float32
    ).astype(jnp.bfloat16)
    return src_grad, cand_grad[:, :width], cand_grad[:, width:]


def on_device(emb, rel, round_key, edge_src, edge_dst, neg_idx, block_count):
    owners = lax.axis_size("grp")
    shard = emb[0]
    copies = jnp.broadcast_to(shard[None], (owners,) + shard.shape)
    table = lax.all_to_all(copies, "grp", 0, 0, tiled=True).reshape(-1, shard.shape[-1])
    rows, depth = table.shape
    scale = depth ** (-0.5)
    sources = edge_src[0, 0]
    targets = edge_dst[0, 0]
    negatives = neg_idx[0, 0]
    counts = block_count[0, 0]
    blocks = sources.shape[0] // 2
    width = sources.shape[1]

    edges = blocks * width
    own_rows = pick_rows(
        table,
        jnp.concatenate(
            [sources.reshape(-1), targets[:blocks].reshape(-1), negatives[:blocks].reshape(-1)]
        ),
    )
    src_rows = own_rows[: 2 * edges]
    query = (
        (src_rows.astype(jnp.float32) * rel * scale)
        .astype(jnp.bfloat16)
        .reshape(2 * blocks, width, depth)
    )
    packed = pack_indices([targets[blocks:], negatives[blocks:]], depth)
    tail = jnp.zeros((32 - packed.shape[0], depth), jnp.bfloat16)
    tail = tail.at[0].set(counts[1].astype(jnp.bfloat16))
    sent = jnp.concatenate([query[blocks:].reshape(-1, depth), packed, tail])
    got = swap_with_partner(sent, round_key[0], "dom")
    got_query = got[: blocks * width].reshape(blocks, width, depth)
    got_pack = got[blocks * width : blocks * width + packed.shape[0]]
    got_dst, got_neg = unpack_indices(got_pack, 2, (blocks, width))
    got_count = got[blocks * width + packed.shape[0], 0:1].astype(jnp.int32)

    sg_a, dg_a, ng_a = block_grads(
        query[:blocks], own_rows[2 * edges : 3 * edges], own_rows[3 * edges :], rel, counts[0]
    )
    got_rows = pick_rows(table, jnp.concatenate([got_dst.reshape(-1), got_neg.reshape(-1)]))
    sg_m, dg_m, ng_m = block_grads(
        got_query, got_rows[:edges], got_rows[edges:], rel, got_count[0]
    )
    sg_b = swap_with_partner(sg_m, round_key[0], "dom")

    where = jnp.concatenate(
        [sources.reshape(-1), targets[:blocks].reshape(-1), negatives[:blocks].reshape(-1),
         got_dst.reshape(-1), got_neg.reshape(-1)]
    )
    grads = jnp.concatenate(
        [g.reshape(-1, depth) for g in (sg_a, sg_b, dg_a, ng_a, dg_m, ng_m)]
    )
    owners = lax.axis_size("grp")
    share = rows // owners
    me = lax.axis_index("grp")
    keep = (jnp.arange(owners, dtype=jnp.int32) == me)[:, None, None]
    part, low = scatter_rows(where, grads, rows)
    part = part.reshape(owners, share, depth)
    got_parts = lax.all_to_all(low.reshape(owners, share, depth), "grp", 0, 0, tiled=True)
    own = lax.dynamic_index_in_dim(part, me, axis=0)
    return jnp.sum(jnp.where(keep, own, got_parts.astype(jnp.float32)), axis=0)[None]


def solution(mesh):
    return jax.shard_map(
        on_device,
        mesh=mesh,
        in_specs=(
            P("dom", "grp", None),
            P(),
            P(),
            P("grp", "dom", None, None),
            P("grp", "dom", None, None),
            P("grp", "dom", None, None),
            P("grp", "dom", None),
        ),
        out_specs=P("dom", "grp", None),
        check_vma=False,
    )
```
